256 devices in a mesh: lat: 16 (over z, core), lon: 16 (over x, y).
Axes of the slice: x: 4, y: 4, z: 8, core: 2. Of those that a mesh axis runs over, the one named last changes fastest.
Arguments:
- east_wind: float32 [4, 4096, 8192], P(None, 'lat', 'lon'), may hold values from -6 to 6
- north_wind: float32 [4, 4096, 8192], P(None, 'lat', 'lon'), may hold values from -6 to 6
- pressure: float32 [4, 4096, 8192], P(None, 'lat', 'lon'), may hold values from -6 to 6
- sound_squared: float32 [4], replicated, may hold values from 0.5 to 2
- column_mass: float32 [4096, 8192], P('lat', 'lon'), may hold values from 0.5 to 1.5
- polar_rows: int32 [512], replicated, may hold values from 0 to 4095, as said below
- cutoffs: int32 [512], replicated, may hold values from 512 to 4095
Outputs:
- new_east: float32 [4, 4096, 8192], P(None, 'lat', 'lon')
- new_north: float32 [4, 4096, 8192], P(None, 'lat', 'lon')
- new_pressure: float32 [4, 4096, 8192], P(None, 'lat', 'lon')
The draws below stay inside these ranges and needn't reach their ends.
Inputs may be any that keep to these rules, and one draw needn't show every extreme that they name: `polar_rows`: distinct rows in ascending order, each poleward of 45 degrees (below 1024 or at least 3072); at most 128 of them lie in one band of 256 rows (rows b * 256 to (b + 1) * 256 - 1), and some band holds exactly 128.
All inputs are finite; a program needn't handle non-finite values.
Results may differ from the reference program's by a relative error of at most 0.00005.
Values sent between devices are 32-bit elements; how exact they have to be, the bound alone decides.
No kernel may reach another device: no remote copies, remote signals or barrier semaphores. Data moves between devices by JAX's collectives and lax.ppermute only.
A program may use at most 64 MiB of HBM per device.

```python
import math
import jax
import jax.numpy as jnp

NLON = 8192
NLAT = 4096
LEVELS = 4
CLAT = 256
KSLOTS = 128
NPOLAR = 512


def draw_polar_rows(key, part):
    band_total = NLAT // CLAT
    polar_bands = band_total // 2
    midway = KSLOTS // 2
    spread = jax.random.randint(jax.random.fold_in(key, 11), (polar_bands // 2,), 0, midway + 1)
    spread = spread.at[0].set(midway)
    counts = jnp.stack([midway + spread, midway - spread], axis=1).reshape(polar_bands)
    band_keys = jax.random.split(jax.random.fold_in(key, 12), polar_bands)
    orders = jax.vmap(lambda one_key: jax.random.permutation(one_key, CLAT))(band_keys)
    chosen = orders < counts[:, None]
    polar_ids = jnp.arange(polar_bands, dtype=jnp.int32)
    band_ids = jnp.where(polar_ids < band_total // 4, polar_ids, polar_ids + band_total // 2)
    global_rows = band_ids[:, None] * CLAT + jnp.arange(CLAT, dtype=jnp.int32)[None, :]
    flags = jnp.zeros((NLAT,), jnp.int32).at[global_rows.reshape(-1)].set(chosen.reshape(-1).astype(jnp.int32))
    return jnp.nonzero(flags, size=NPOLAR)[0].astype(jnp.int32)


def with_ends(result, rng, low, largest):
    longest = result.shape.index(max(result.shape))
    spots = []
    for shift in (0, 1):
        where = [jax.random.randint(jax.random.fold_in(rng, axis), (), 0, length) for axis, length in enumerate(result.shape)]
        where[longest] = (where[longest] + shift) % result.shape[longest]
        spots.append(tuple(where))
    return result.at[spots[0]].set(low).at[spots[1]].set(largest)


def shard_levels(key, dims, shards, least, top_value):
    gain, own = 1.0, jax.random.fold_in(key, 6)
    for axis_at, shards_of in shards:
        draws = jnp.exp(jax.random.uniform(jax.random.fold_in(own, axis_at), (shards_of,), jnp.float32, least / len(shards), top_value / len(shards)))
        gain = gain * jnp.repeat(draws, dims[axis_at] // shards_of).reshape([-1 if axis == axis_at else 1 for axis in range(len(dims))])
    return gain


def bell_draw(own_key, extent, scale, reach, shards=(), kind=jnp.bfloat16):
    array = scale * jax.random.normal(own_key, extent, jnp.float32)
    if shards:
        array = array * shard_levels(own_key, extent, shards, -0.22, 0.18)
    return jnp.clip(array, -reach, reach).astype(kind)


def setup_inputs(seed: int = 0) -> dict:
    key_list = jax.random.split(jax.random.key(seed), 8)
    east_wind = bell_draw(key_list[0], (LEVELS, NLAT, NLON), 1.0, 6.0, ((1, 16), (2, 16)), jnp.float32)
    north_wind = bell_draw(key_list[1], (LEVELS, NLAT, NLON), 1.0, 6.0, ((1, 16), (2, 16)), jnp.float32)
    pressure = bell_draw(key_list[2], (LEVELS, NLAT, NLON), 1.0, 6.0, ((1, 16), (2, 16)), jnp.float32)
    sound_squared = jnp.clip(jnp.exp(jax.random.uniform(key_list[3], (LEVELS,), jnp.float32, math.log(0.5), math.log(2.0))), 0.5, 2.0)
    column_mass = jnp.clip(0.5 + 1.0 * jax.random.uniform(key_list[4], (NLAT, NLON), jnp.float32) ** shard_levels(key_list[4], (NLAT, NLON), ((0, 16), (1, 16)), -0.2, 0.2), 0.5, 1.5)
    polar_rows = draw_polar_rows(jax.random.fold_in(key_list[7], 71), 0)
    cutoffs = with_ends(jax.random.randint(key_list[6], (NPOLAR,), NLON // 16, NLON // 2), jax.random.fold_in(key_list[6], 1), NLON // 16, (NLON // 2) - 1).astype(jnp.int32)
    return {"east_wind": east_wind, "north_wind": north_wind, "pressure": pressure, "sound_squared": sound_squared, "column_mass": column_mass, "polar_rows": polar_rows, "cutoffs": cutoffs}


def latitude_terms(global_rows, total_rows):
    latitude = (-0.5 + (global_rows.astype(jnp.float32) + 0.5) / total_rows) * jnp.pi
    cosine = jnp.cos(latitude)
    courant = 0.3 * jnp.minimum(1.0 / cosine, 2.0)
    return cosine, courant


def reference(east_wind, north_wind, pressure, sound_squared, column_mass, polar_rows, cutoffs):
    cosine, courant = latitude_terms(jnp.arange(NLAT, dtype=jnp.int32), NLAT)
    lat_factor = courant[None, :, None]
    blank = jnp.zeros((LEVELS, 1, NLON), pressure.dtype)
    east = jnp.roll(pressure, -1, axis=2)
    west = jnp.roll(pressure, 1, axis=2)
    north = jnp.concatenate([pressure[:, 1:], blank], axis=1)
    south = jnp.concatenate([blank, pressure[:, :-1]], axis=1)
    east_step = east_wind - lat_factor * (east - west) * 0.5
    north_step = north_wind - 0.3 * (north - south) * 0.5
    stacked = jnp.stack([east_step, north_step])
    chosen = stacked[:, :, polar_rows, :]
    spectrum = jnp.fft.fft(chosen, axis=-1)
    waves = jnp.arange(NLON, dtype=jnp.int32)
    waves = jnp.minimum(waves, NLON - waves)
    keeping = waves[None, :] <= cutoffs[:, None]
    spectrum = jnp.where(keeping[None, None], spectrum, jnp.zeros_like(spectrum))
    smoothed = jnp.real(jnp.fft.ifft(spectrum, axis=-1)).astype(pressure.dtype)
    updated = stacked.at[:, :, polar_rows, :].set(smoothed)
    new_east = updated[0]
    new_north = updated[1]
    carried = new_north * cosine[None, :, None]
    east_u = jnp.roll(new_east, -1, axis=2)
    west_u = jnp.roll(new_east, 1, axis=2)
    north_v = jnp.concatenate([carried[:, 1:], blank], axis=1)
    south_v = jnp.concatenate([blank, carried[:, :-1]], axis=1)
    divergence = lat_factor * (east_u - west_u) * 0.5 + 0.3 * (north_v - south_v) * 0.5 / cosine[None, :, None]
    new_pressure = pressure - sound_squared[:, None, None] * divergence / column_mass[None]
    return new_east, new_north, new_pressure
```

```python
import jax
import jax.numpy as jnp
from jax import lax
from jax.experimental import pallas as pl
from jax.experimental.pallas import tpu as pltpu
from jax.sharding import PartitionSpec as P

PRECISE = lax.Precision.HIGHEST


def shift_pairs(peers, step, wrap):
    pairs = []
    for i in range(peers):
        j = i + step
        if wrap:
            pairs.append((i, j % peers))
        elif 0 <= j < peers:
            pairs.append((i, j))
    return pairs


def halos(lat_first, lat_last, lon_first, lon_last):
    bands = lax.axis_size("lat")
    segs = lax.axis_size("lon")
    north = lax.ppermute(lat_first, "lat", shift_pairs(bands, -1, False))
    south = lax.ppermute(lat_last, "lat", shift_pairs(bands, 1, False))
    east = lax.ppermute(lon_first, "lon", shift_pairs(segs, -1, True))
    west = lax.ppermute(lon_last, "lon", shift_pairs(segs, 1, True))
    return north, south, east, west


def latitude_terms(global_rows, total_rows):
    latitude = (-0.5 + (global_rows.astype(jnp.float32) + 0.5) / total_rows) * jnp.pi
    cosine = jnp.cos(latitude)
    courant = 0.3 * jnp.minimum(1.0 / cosine, 2.0)
    return (cosine, courant)


def slot_table(polar_rows, cutoffs, band_number, row_count, slot_count):
    lower = band_number * row_count
    rows = jnp.arange(row_count, dtype=jnp.int32)
    listed = jnp.any(polar_rows[None, :] == (lower + rows)[:, None], axis=1)
    count = jnp.sum(listed.astype(jnp.int32))
    order = jnp.argsort(jnp.where(listed, rows, rows + row_count))
    targets = order[:slot_count].astype(jnp.int32)
    opening = jnp.sum((polar_rows < lower).astype(jnp.int32))
    slots = jnp.arange(slot_count, dtype=jnp.int32)
    present = slots < count
    safe_entries = jnp.clip(opening + slots, 0, polar_rows.shape[0] - 1)
    limits = jnp.take(cutoffs, safe_entries)
    return present, targets, limits


def gather_rows(rows, east, north):
    levels, _, width = east.shape
    slot_count = rows.shape[0]

    def kernel(rows_ref, east_hbm, north_hbm, out_hbm, sem):
        def body(s, carry):
            r = rows_ref[s]
            pltpu.make_async_copy(
                east_hbm.at[:, r, :], out_hbm.at[s, pl.ds(0, levels), :], sem
            ).start()
            pltpu.make_async_copy(
                north_hbm.at[:, r, :], out_hbm.at[s, pl.ds(levels, levels), :], sem
            ).start()
            return carry

        lax.fori_loop(0, slot_count, body, 0)
        pltpu.make_async_copy(out_hbm, out_hbm, sem).wait()

    return pl.pallas_call(
        kernel,
        out_shape=jax.ShapeDtypeStruct((slot_count, 2 * levels, width), east.dtype),
        grid_spec=pltpu.PrefetchScalarGridSpec(
            num_scalar_prefetch=1,
            grid=(1,),
            in_specs=[pl.BlockSpec(memory_space=pl.ANY), pl.BlockSpec(memory_space=pl.ANY)],
            out_specs=pl.BlockSpec(memory_space=pl.ANY),
            scratch_shapes=[pltpu.SemaphoreType.DMA(())],
        ),
    )(rows, east, north)


def scatter_rows(rows, slots, east, north):
    levels, _, width = east.shape
    slot_count = rows.shape[0]

    def kernel(rows_ref, slots_hbm, east_in, north_in, east_hbm, north_hbm, sem):
        def body(s, carry):
            r = rows_ref[s]
            pltpu.make_async_copy(
                slots_hbm.at[s, pl.ds(0, levels), :], east_hbm.at[:, r, :], sem
            ).start()
            pltpu.make_async_copy(
                slots_hbm.at[s, pl.ds(levels, levels), :], north_hbm.at[:, r, :], sem
            ).start()
            return carry

        lax.fori_loop(0, slot_count, body, 0)
        pltpu.make_async_copy(slots_hbm, slots_hbm, sem).wait()

    return pl.pallas_call(
        kernel,
        out_shape=(
            jax.ShapeDtypeStruct(east.shape, east.dtype),
            jax.ShapeDtypeStruct(north.shape, north.dtype),
        ),
        grid_spec=pltpu.PrefetchScalarGridSpec(
            num_scalar_prefetch=1,
            grid=(1,),
            in_specs=[pl.BlockSpec(memory_space=pl.ANY)] * 3,
            out_specs=(pl.BlockSpec(memory_space=pl.ANY), pl.BlockSpec(memory_space=pl.ANY)),
            scratch_shapes=[pltpu.SemaphoreType.DMA(())],
        ),
        input_output_aliases={2: 0, 3: 1},
    )(rows, slots, east, north)


def dft_filter(row_data, limits):
    row_total, length = row_data.shape
    inner = 128
    outer = length // inner
    outer_ids = jnp.arange(outer, dtype=jnp.int32)
    inner_ids = jnp.arange(inner, dtype=jnp.int32)
    angle_one = (
        2.0 * jnp.pi * (outer_ids[:, None] * outer_ids[None, :] % outer).astype(jnp.float32) / outer
    )
    angle_two = (
        2.0 * jnp.pi * (inner_ids[:, None] * inner_ids[None, :] % inner).astype(jnp.float32) / inner
    )
    angle_twist = (
        2.0
        * jnp.pi
        * (outer_ids[:, None] * inner_ids[None, :] % length).astype(jnp.float32)
        / length
    )
    cos_one, sin_one = (jnp.cos(angle_one), jnp.sin(angle_one))
    cos_two, sin_two = (jnp.cos(angle_two), jnp.sin(angle_two))
    cos_twist, sin_twist = (jnp.cos(angle_twist), jnp.sin(angle_twist))
    folded = row_data.reshape(row_total, outer, inner)
    real_a = jnp.einsum("mab,ak->mkb", folded, cos_one, precision=PRECISE)
    imag_a = -jnp.einsum("mab,ak->mkb", folded, sin_one, precision=PRECISE)
    real_b = real_a * cos_twist + imag_a * sin_twist
    imag_b = imag_a * cos_twist - real_a * sin_twist
    real_c = jnp.einsum("mkb,bj->mkj", real_b, cos_two, precision=PRECISE) + jnp.einsum(
        "mkb,bj->mkj", imag_b, sin_two, precision=PRECISE
    )
    imag_c = jnp.einsum("mkb,bj->mkj", imag_b, cos_two, precision=PRECISE) - jnp.einsum(
        "mkb,bj->mkj", real_b, sin_two, precision=PRECISE
    )
    wave_ids = outer_ids[:, None] + outer * inner_ids[None, :]
    wave_ids = jnp.minimum(wave_ids, length - wave_ids)
    keeping = (wave_ids[None] <= limits[:, None, None]).astype(jnp.float32)
    real_c = real_c * keeping
    imag_c = imag_c * keeping
    real_d = jnp.einsum("mkj,jb->mkb", real_c, cos_two, precision=PRECISE) - jnp.einsum(
        "mkj,jb->mkb", imag_c, sin_two, precision=PRECISE
    )
    imag_d = jnp.einsum("mkj,jb->mkb", imag_c, cos_two, precision=PRECISE) + jnp.einsum(
        "mkj,jb->mkb", real_c, sin_two, precision=PRECISE
    )
    real_e = real_d * cos_twist - imag_d * sin_twist
    imag_e = imag_d * cos_twist + real_d * sin_twist
    result = jnp.einsum("mkb,ka->mab", real_e, cos_one, precision=PRECISE) - jnp.einsum(
        "mkb,ka->mab", imag_e, sin_one, precision=PRECISE
    )
    return (result / length).reshape(row_total, length)


def filter_round(slots, slot_limits):
    slot_total, per_slot, seg_width = slots.shape
    items = slots.reshape(slot_total * per_slot, seg_width)
    whole_rows = lax.all_to_all(items, "lon", split_axis=0, concat_axis=1, tiled=True)
    share = whole_rows.shape[0]
    item_ids = lax.axis_index("lon") * share + jnp.arange(share, dtype=jnp.int32)
    item_limits = jnp.take(slot_limits, item_ids // per_slot)
    filtered = dft_filter(whole_rows, item_limits)
    returned = lax.all_to_all(filtered, "lon", split_axis=1, concat_axis=0, tiled=True)
    return returned.reshape(slot_total, per_slot, seg_width)


def shifted(block, before, after, axis):
    length = block.shape[axis]
    plus = jnp.concatenate([lax.slice_in_dim(block, 1, length, axis=axis), after], axis=axis)
    minus = jnp.concatenate([before, lax.slice_in_dim(block, 0, length - 1, axis=axis)], axis=axis)
    return plus, minus


def on_device(east_wind, north_wind, pressure, sound_squared, column_mass, polar_rows, cutoffs):
    level_count, row_count, seg_width = pressure.shape
    band_count = lax.axis_size("lat")
    band_number = lax.axis_index("lat")
    total_rows = row_count * band_count
    global_rows = band_number * row_count + jnp.arange(row_count, dtype=jnp.int32)
    cosine, courant = latitude_terms(global_rows, total_rows)
    lat_factor = courant[None, :, None]

    p_north, p_south, p_east, p_west = halos(
        pressure[:, 0, :], pressure[:, -1, :], pressure[:, :, 0], pressure[:, :, -1]
    )
    east, west = shifted(pressure, p_west[:, :, None], p_east[:, :, None], 2)
    north, south = shifted(pressure, p_south[:, None, :], p_north[:, None, :], 1)
    east_step = east_wind - lat_factor * (east - west) * 0.5
    north_step = north_wind - 0.3 * (north - south) * 0.5

    slot_count = row_count // 2
    present, targets, limits = slot_table(polar_rows, cutoffs, band_number, row_count, slot_count)
    picked = gather_rows(targets, east_step, north_step)
    whole_limit = seg_width * lax.axis_size("lon") // 2
    smoothed = filter_round(picked, jnp.where(present, limits, whole_limit))
    smoothed = jnp.where(present[:, None, None], smoothed, picked)
    new_east, new_north = scatter_rows(targets, smoothed, east_step, north_step)

    carried = new_north * cosine[None, :, None]
    v_north, v_south, u_east, u_west = halos(
        carried[:, 0, :], carried[:, -1, :], new_east[:, :, 0], new_east[:, :, -1]
    )
    east_u, west_u = shifted(new_east, u_west[:, :, None], u_east[:, :, None], 2)
    north_v, south_v = shifted(carried, v_south[:, None, :], v_north[:, None, :], 1)
    divergence = (
        lat_factor * (east_u - west_u) * 0.5
        + 0.3 * (north_v - south_v) * 0.5 / cosine[None, :, None]
    )
    new_pressure = pressure - sound_squared[:, None, None] * divergence / column_mass[None]
    return (new_east, new_north, new_pressure)


def solution(mesh):
    in_specs = (
        P(None, "lat", "lon"),
        P(None, "lat", "lon"),
        P(None, "lat", "lon"),
        P(),
        P("lat", "lon"),
        P(),
        P(),
    )
    out_specs = (P(None, "lat", "lon"), P(None, "lat", "lon"), P(None, "lat", "lon"))
    return jax.shard_map(
        on_device, mesh=mesh, in_specs=in_specs, out_specs=out_specs, check_vma=False
    )
```

```python
import jax
import jax.numpy as jnp
from jax import lax
from jax.sharding import PartitionSpec as P

PRECISE = lax.Precision.HIGHEST


def shift_pairs(peers, step, wrap):
    pairs = []
    for i in range(peers):
        j = i + step
        if wrap:
            pairs.append((i, j % peers))
        elif 0 <= j < peers:
            pairs.append((i, j))
    return pairs


def halos(lat_first, lat_last, lon_first, lon_last):
    bands = lax.axis_size("lat")
    segs = lax.axis_size("lon")
    north = lax.ppermute(lat_first, "lat", shift_pairs(bands, -1, False))
    south = lax.ppermute(lat_last, "lat", shift_pairs(bands, 1, False))
    east = lax.ppermute(lon_first, "lon", shift_pairs(segs, -1, True))
    west = lax.ppermute(lon_last, "lon", shift_pairs(segs, 1, True))
    return north, south, east, west


def latitude_terms(global_rows, total_rows):
    latitude = (-0.5 + (global_rows.astype(jnp.float32) + 0.5) / total_rows) * jnp.pi
    cosine = jnp.cos(latitude)
    courant = 0.3 * jnp.minimum(1.0 / cosine, 2.0)
    return (cosine, courant)


def slot_table(polar_rows, cutoffs, band_number, row_count, slot_count):
    lower = band_number * row_count
    opening = jnp.sum((polar_rows < lower).astype(jnp.int32))
    closing = jnp.sum((polar_rows < lower + row_count).astype(jnp.int32))
    entries = opening + jnp.arange(slot_count, dtype=jnp.int32)
    present = entries < closing
    safe_entries = jnp.clip(entries, 0, polar_rows.shape[0] - 1)
    local_rows = jnp.take(polar_rows, safe_entries) - lower
    limits = jnp.take(cutoffs, safe_entries)
    rows = jnp.arange(row_count, dtype=jnp.int32)
    choice = ((local_rows[:, None] == rows[None, :]) & present[:, None]).astype(jnp.float32)
    return (present, choice, limits)


def dft_filter(row_data, limits):
    row_total, length = row_data.shape
    inner = 128
    outer = length // inner
    outer_ids = jnp.arange(outer, dtype=jnp.int32)
    inner_ids = jnp.arange(inner, dtype=jnp.int32)
    angle_one = (
        2.0 * jnp.pi * (outer_ids[:, None] * outer_ids[None, :] % outer).astype(jnp.float32) / outer
    )
    angle_two = (
        2.0 * jnp.pi * (inner_ids[:, None] * inner_ids[None, :] % inner).astype(jnp.float32) / inner
    )
    angle_twist = (
        2.0
        * jnp.pi
        * (outer_ids[:, None] * inner_ids[None, :] % length).astype(jnp.float32)
        / length
    )
    cos_one, sin_one = (jnp.cos(angle_one), jnp.sin(angle_one))
    cos_two, sin_two = (jnp.cos(angle_two), jnp.sin(angle_two))
    cos_twist, sin_twist = (jnp.cos(angle_twist), jnp.sin(angle_twist))
    folded = row_data.reshape(row_total, outer, inner)
    real_a = jnp.einsum("mab,ak->mkb", folded, cos_one, precision=PRECISE)
    imag_a = -jnp.einsum("mab,ak->mkb", folded, sin_one, precision=PRECISE)
    real_b = real_a * cos_twist + imag_a * sin_twist
    imag_b = imag_a * cos_twist - real_a * sin_twist
    real_c = jnp.einsum("mkb,bj->mkj", real_b, cos_two, precision=PRECISE) + jnp.einsum(
        "mkb,bj->mkj", imag_b, sin_two, precision=PRECISE
    )
    imag_c = jnp.einsum("mkb,bj->mkj", imag_b, cos_two, precision=PRECISE) - jnp.einsum(
        "mkb,bj->mkj", real_b, sin_two, precision=PRECISE
    )
    wave_ids = outer_ids[:, None] + outer * inner_ids[None, :]
    wave_ids = jnp.minimum(wave_ids, length - wave_ids)
    keeping = (wave_ids[None] <= limits[:, None, None]).astype(jnp.float32)
    real_c = real_c * keeping
    imag_c = imag_c * keeping
    real_d = jnp.einsum("mkj,jb->mkb", real_c, cos_two, precision=PRECISE) - jnp.einsum(
        "mkj,jb->mkb", imag_c, sin_two, precision=PRECISE
    )
    imag_d = jnp.einsum("mkj,jb->mkb", imag_c, cos_two, precision=PRECISE) + jnp.einsum(
        "mkj,jb->mkb", real_c, sin_two, precision=PRECISE
    )
    real_e = real_d * cos_twist - imag_d * sin_twist
    imag_e = imag_d * cos_twist + real_d * sin_twist
    result = jnp.einsum("mkb,ka->mab", real_e, cos_one, precision=PRECISE) - jnp.einsum(
        "mkb,ka->mab", imag_e, sin_one, precision=PRECISE
    )
    return (result / length).reshape(row_total, length)


def filter_round(slots, slot_limits):
    slot_total, per_slot, seg_width = slots.shape
    items = slots.reshape(slot_total * per_slot, seg_width)
    whole_rows = lax.all_to_all(items, "lon", split_axis=0, concat_axis=1, tiled=True)
    share = whole_rows.shape[0]
    item_ids = lax.axis_index("lon") * share + jnp.arange(share, dtype=jnp.int32)
    item_limits = jnp.take(slot_limits, item_ids // per_slot)
    filtered = dft_filter(whole_rows, item_limits)
    returned = lax.all_to_all(filtered, "lon", split_axis=1, concat_axis=0, tiled=True)
    return returned.reshape(slot_total, per_slot, seg_width)


def shifted(block, before, after, axis):
    length = block.shape[axis]
    plus = jnp.concatenate([lax.slice_in_dim(block, 1, length, axis=axis), after], axis=axis)
    minus = jnp.concatenate([before, lax.slice_in_dim(block, 0, length - 1, axis=axis)], axis=axis)
    return plus, minus


def on_device(east_wind, north_wind, pressure, sound_squared, column_mass, polar_rows, cutoffs):
    level_count, row_count, seg_width = pressure.shape
    band_count = lax.axis_size("lat")
    band_number = lax.axis_index("lat")
    total_rows = row_count * band_count
    global_rows = band_number * row_count + jnp.arange(row_count, dtype=jnp.int32)
    cosine, courant = latitude_terms(global_rows, total_rows)
    lat_factor = courant[None, :, None]

    p_north, p_south, p_east, p_west = halos(
        pressure[:, 0, :], pressure[:, -1, :], pressure[:, :, 0], pressure[:, :, -1]
    )
    east, west = shifted(pressure, p_west[:, :, None], p_east[:, :, None], 2)
    north, south = shifted(pressure, p_south[:, None, :], p_north[:, None, :], 1)
    east_step = east_wind - lat_factor * (east - west) * 0.5
    north_step = north_wind - 0.3 * (north - south) * 0.5

    slot_count = row_count // 2
    present, choice, limits = slot_table(polar_rows, cutoffs, band_number, row_count, slot_count)
    stacked = jnp.concatenate([east_step, north_step], axis=0)
    picked = jnp.einsum("sr,frc->sfc", choice, stacked, precision=PRECISE)
    whole_limit = seg_width * lax.axis_size("lon") // 2
    smoothed = filter_round(picked, jnp.where(present, limits, whole_limit))
    placed = jnp.einsum("sr,sfc->frc", choice, smoothed, precision=PRECISE)
    listed = jnp.sum(choice, axis=0) > 0.5
    updated = jnp.where(listed[None, :, None], placed, stacked)
    new_east = updated[:level_count]
    new_north = updated[level_count:]

    carried = new_north * cosine[None, :, None]
    v_north, v_south, u_east, u_west = halos(
        carried[:, 0, :], carried[:, -1, :], new_east[:, :, 0], new_east[:, :, -1]
    )
    east_u, west_u = shifted(new_east, u_west[:, :, None], u_east[:, :, None], 2)
    north_v, south_v = shifted(carried, v_south[:, None, :], v_north[:, None, :], 1)
    divergence = (
        lat_factor * (east_u - west_u) * 0.5
        + 0.3 * (north_v - south_v) * 0.5 / cosine[None, :, None]
    )
    new_pressure = pressure - sound_squared[:, None, None] * divergence / column_mass[None]
    return (new_east, new_north, new_pressure)


def solution(mesh):
    in_specs = (
        P(None, "lat", "lon"),
        P(None, "lat", "lon"),
        P(None, "lat", "lon"),
        P(),
        P("lat", "lon"),
        P(),
        P(),
    )
    out_specs = (P(None, "lat", "lon"), P(None, "lat", "lon"), P(None, "lat", "lon"))
    return jax.shard_map(
        on_device, mesh=mesh, in_specs=in_specs, out_specs=out_specs, check_vma=False
    )
```

```python
import jax
import jax.numpy as jnp
from jax import lax
from jax.sharding import PartitionSpec as P

PRECISE = lax.Precision.HIGHEST
FILTER_CHUNKS = 2


def shift_pairs(peers, step, wrap):
    pairs = []
    for i in range(peers):
        j = i + step
        if wrap:
            pairs.append((i, j % peers))
        elif 0 <= j < peers:
            pairs.append((i, j))
    return pairs


def halos(lat_first, lat_last, lon_first, lon_last):
    bands = lax.axis_size("lat")
    segs = lax.axis_size("lon")
    north = lax.ppermute(lat_first, "lat", shift_pairs(bands, -1, False))
    south = lax.ppermute(lat_last, "lat", shift_pairs(bands, 1, False))
    east = lax.ppermute(lon_first, "lon", shift_pairs(segs, -1, True))
    west = lax.ppermute(lon_last, "lon", shift_pairs(segs, 1, True))
    return north, south, east, west


def latitude_terms(global_rows, total_rows):
    latitude = (-0.5 + (global_rows.astype(jnp.float32) + 0.5) / total_rows) * jnp.pi
    cosine = jnp.cos(latitude)
    courant = 0.3 * jnp.minimum(1.0 / cosine, 2.0)
    return (cosine, courant)


def slot_table(polar_rows, cutoffs, band_number, row_count, slot_count):
    lower = band_number * row_count
    opening = jnp.sum((polar_rows < lower).astype(jnp.int32))
    closing = jnp.sum((polar_rows < lower + row_count).astype(jnp.int32))
    entries = opening + jnp.arange(slot_count, dtype=jnp.int32)
    present = entries < closing
    safe_entries = jnp.clip(entries, 0, polar_rows.shape[0] - 1)
    local_rows = jnp.take(polar_rows, safe_entries) - lower
    limits = jnp.take(cutoffs, safe_entries)
    rows = jnp.arange(row_count, dtype=jnp.int32)
    choice = ((local_rows[:, None] == rows[None, :]) & present[:, None]).astype(jnp.float32)
    return (present, choice, limits)


def dft_filter(row_data, limits):
    row_total, length = row_data.shape
    inner = 128
    outer = length // inner
    outer_ids = jnp.arange(outer, dtype=jnp.int32)
    inner_ids = jnp.arange(inner, dtype=jnp.int32)
    angle_one = (
        2.0 * jnp.pi * (outer_ids[:, None] * outer_ids[None, :] % outer).astype(jnp.float32) / outer
    )
    angle_two = (
        2.0 * jnp.pi * (inner_ids[:, None] * inner_ids[None, :] % inner).astype(jnp.float32) / inner
    )
    angle_twist = (
        2.0
        * jnp.pi
        * (outer_ids[:, None] * inner_ids[None, :] % length).astype(jnp.float32)
        / length
    )
    cos_one, sin_one = (jnp.cos(angle_one), jnp.sin(angle_one))
    cos_two, sin_two = (jnp.cos(angle_two), jnp.sin(angle_two))
    cos_twist, sin_twist = (jnp.cos(angle_twist), jnp.sin(angle_twist))
    folded = row_data.reshape(row_total, outer, inner)
    real_a = jnp.einsum("mab,ak->mkb", folded, cos_one, precision=PRECISE)
    imag_a = -jnp.einsum("mab,ak->mkb", folded, sin_one, precision=PRECISE)
    real_b = real_a * cos_twist + imag_a * sin_twist
    imag_b = imag_a * cos_twist - real_a * sin_twist
    real_c = jnp.einsum("mkb,bj->mkj", real_b, cos_two, precision=PRECISE) + jnp.einsum(
        "mkb,bj->mkj", imag_b, sin_two, precision=PRECISE
    )
    imag_c = jnp.einsum("mkb,bj->mkj", imag_b, cos_two, precision=PRECISE) - jnp.einsum(
        "mkb,bj->mkj", real_b, sin_two, precision=PRECISE
    )
    wave_ids = outer_ids[:, None] + outer * inner_ids[None, :]
    wave_ids = jnp.minimum(wave_ids, length - wave_ids)
    keeping = (wave_ids[None] <= limits[:, None, None]).astype(jnp.float32)
    real_c = real_c * keeping
    imag_c = imag_c * keeping
    real_d = jnp.einsum("mkj,jb->mkb", real_c, cos_two, precision=PRECISE) - jnp.einsum(
        "mkj,jb->mkb", imag_c, sin_two, precision=PRECISE
    )
    imag_d = jnp.einsum("mkj,jb->mkb", imag_c, cos_two, precision=PRECISE) + jnp.einsum(
        "mkj,jb->mkb", real_c, sin_two, precision=PRECISE
    )
    real_e = real_d * cos_twist - imag_d * sin_twist
    imag_e = imag_d * cos_twist + real_d * sin_twist
    result = jnp.einsum("mkb,ka->mab", real_e, cos_one, precision=PRECISE) - jnp.einsum(
        "mkb,ka->mab", imag_e, sin_one, precision=PRECISE
    )
    return (result / length).reshape(row_total, length)


def filter_round(slots, slot_limits, chunks):
    slot_total, per_slot, seg_width = slots.shape
    chunk_slots = slot_total // chunks
    pieces = []
    for c in range(chunks):
        part = lax.slice_in_dim(slots, c * chunk_slots, (c + 1) * chunk_slots, axis=0)
        items = part.reshape(chunk_slots * per_slot, seg_width)
        whole_rows = lax.all_to_all(items, "lon", split_axis=0, concat_axis=1, tiled=True)
        share = whole_rows.shape[0]
        item_ids = lax.axis_index("lon") * share + jnp.arange(share, dtype=jnp.int32)
        item_limits = jnp.take(slot_limits, c * chunk_slots + item_ids // per_slot)
        filtered = dft_filter(whole_rows, item_limits)
        returned = lax.all_to_all(filtered, "lon", split_axis=1, concat_axis=0, tiled=True)
        pieces.append(returned.reshape(chunk_slots, per_slot, seg_width))
    return jnp.concatenate(pieces, axis=0)


def shifted(block, before, after, axis):
    length = block.shape[axis]
    plus = jnp.concatenate([lax.slice_in_dim(block, 1, length, axis=axis), after], axis=axis)
    minus = jnp.concatenate([before, lax.slice_in_dim(block, 0, length - 1, axis=axis)], axis=axis)
    return plus, minus


def on_device(east_wind, north_wind, pressure, sound_squared, column_mass, polar_rows, cutoffs):
    level_count, row_count, seg_width = pressure.shape
    band_count = lax.axis_size("lat")
    band_number = lax.axis_index("lat")
    total_rows = row_count * band_count
    global_rows = band_number * row_count + jnp.arange(row_count, dtype=jnp.int32)
    cosine, courant = latitude_terms(global_rows, total_rows)
    lat_factor = courant[None, :, None]

    p_north, p_south, p_east, p_west = halos(
        pressure[:, 0, :], pressure[:, -1, :], pressure[:, :, 0], pressure[:, :, -1]
    )
    east, west = shifted(pressure, p_west[:, :, None], p_east[:, :, None], 2)
    north, south = shifted(pressure, p_south[:, None, :], p_north[:, None, :], 1)
    east_step = east_wind - lat_factor * (east - west) * 0.5
    north_step = north_wind - 0.3 * (north - south) * 0.5

    slot_count = row_count // 2
    present, choice, limits = slot_table(polar_rows, cutoffs, band_number, row_count, slot_count)
    stacked = jnp.concatenate([east_step, north_step], axis=0)
    picked = jnp.einsum("sr,frc->sfc", choice, stacked, precision=PRECISE)
    whole_limit = seg_width * lax.axis_size("lon") // 2
    smoothed = filter_round(picked, jnp.where(present, limits, whole_limit), FILTER_CHUNKS)
    placed = jnp.einsum("sr,sfc->frc", choice, smoothed, precision=PRECISE)
    listed = jnp.sum(choice, axis=0) > 0.5
    updated = jnp.where(listed[None, :, None], placed, stacked)
    new_east = updated[:level_count]
    new_north = updated[level_count:]

    carried = new_north * cosine[None, :, None]
    v_north, v_south, u_east, u_west = halos(
        carried[:, 0, :], carried[:, -1, :], new_east[:, :, 0], new_east[:, :, -1]
    )
    east_u, west_u = shifted(new_east, u_west[:, :, None], u_east[:, :, None], 2)
    north_v, south_v = shifted(carried, v_south[:, None, :], v_north[:, None, :], 1)
    divergence = (
        lat_factor * (east_u - west_u) * 0.5
        + 0.3 * (north_v - south_v) * 0.5 / cosine[None, :, None]
    )
    new_pressure = pressure - sound_squared[:, None, None] * divergence / column_mass[None]
    return (new_east, new_north, new_pressure)


def solution(mesh):
    in_specs = (
        P(None, "lat", "lon"),
        P(None, "lat", "lon"),
        P(None, "lat", "lon"),
        P(),
        P("lat", "lon"),
        P(),
        P(),
    )
    out_specs = (P(None, "lat", "lon"), P(None, "lat", "lon"), P(None, "lat", "lon"))
    return jax.shard_map(
        on_device, mesh=mesh, in_specs=in_specs, out_specs=out_specs, check_vma=False
    )
```

```python
import jax
import jax.numpy as jnp
from jax import lax
from jax.sharding import PartitionSpec as P

PRECISE = lax.Precision.HIGHEST
SPECTRAL = lax.Precision.HIGH


def shift_pairs(peers, step, wrap):
    pairs = []
    for i in range(peers):
        j = i + step
        if wrap:
            pairs.append((i, j % peers))
        elif 0 <= j < peers:
            pairs.append((i, j))
    return pairs


def halos(lat_first, lat_last, lon_first, lon_last):
    bands = lax.axis_size("lat")
    segs = lax.axis_size("lon")
    north = lax.ppermute(lat_first, "lat", shift_pairs(bands, -1, False))
    south = lax.ppermute(lat_last, "lat", shift_pairs(bands, 1, False))
    east = lax.ppermute(lon_first, "lon", shift_pairs(segs, -1, True))
    west = lax.ppermute(lon_last, "lon", shift_pairs(segs, 1, True))
    return north, south, east, west


def latitude_terms(global_rows, total_rows):
    latitude = (-0.5 + (global_rows.astype(jnp.float32) + 0.5) / total_rows) * jnp.pi
    cosine = jnp.cos(latitude)
    courant = 0.3 * jnp.minimum(1.0 / cosine, 2.0)
    return (cosine, courant)


def slot_table(polar_rows, cutoffs, band_number, row_count, slot_count):
    lower = band_number * row_count
    opening = jnp.sum((polar_rows < lower).astype(jnp.int32))
    closing = jnp.sum((polar_rows < lower + row_count).astype(jnp.int32))
    entries = opening + jnp.arange(slot_count, dtype=jnp.int32)
    present = entries < closing
    safe_entries = jnp.clip(entries, 0, polar_rows.shape[0] - 1)
    local_rows = jnp.take(polar_rows, safe_entries) - lower
    limits = jnp.take(cutoffs, safe_entries)
    rows = jnp.arange(row_count, dtype=jnp.int32)
    choice = ((local_rows[:, None] == rows[None, :]) & present[:, None]).astype(jnp.float32)
    return (present, choice, limits)


def dft_filter(row_data, limits):
    row_total, length = row_data.shape
    inner = 128
    outer = length // inner
    outer_ids = jnp.arange(outer, dtype=jnp.int32)
    inner_ids = jnp.arange(inner, dtype=jnp.int32)
    angle_one = (
        2.0 * jnp.pi * (outer_ids[:, None] * outer_ids[None, :] % outer).astype(jnp.float32) / outer
    )
    angle_two = (
        2.0 * jnp.pi * (inner_ids[:, None] * inner_ids[None, :] % inner).astype(jnp.float32) / inner
    )
    angle_twist = (
        2.0
        * jnp.pi
        * (outer_ids[:, None] * inner_ids[None, :] % length).astype(jnp.float32)
        / length
    )
    cos_one, sin_one = (jnp.cos(angle_one), jnp.sin(angle_one))
    cos_two, sin_two = (jnp.cos(angle_two), jnp.sin(angle_two))
    cos_twist, sin_twist = (jnp.cos(angle_twist), jnp.sin(angle_twist))
    folded = row_data.reshape(row_total, outer, inner)
    real_a = jnp.einsum("mab,ak->mkb", folded, cos_one, precision=SPECTRAL)
    imag_a = -jnp.einsum("mab,ak->mkb", folded, sin_one, precision=SPECTRAL)
    real_b = real_a * cos_twist + imag_a * sin_twist
    imag_b = imag_a * cos_twist - real_a * sin_twist
    real_c = jnp.einsum("mkb,bj->mkj", real_b, cos_two, precision=SPECTRAL) + jnp.einsum(
        "mkb,bj->mkj", imag_b, sin_two, precision=SPECTRAL
    )
    imag_c = jnp.einsum("mkb,bj->mkj", imag_b, cos_two, precision=SPECTRAL) - jnp.einsum(
        "mkb,bj->mkj", real_b, sin_two, precision=SPECTRAL
    )
    wave_ids = outer_ids[:, None] + outer * inner_ids[None, :]
    wave_ids = jnp.minimum(wave_ids, length - wave_ids)
    keeping = (wave_ids[None] <= limits[:, None, None]).astype(jnp.float32)
    real_c = real_c * keeping
    imag_c = imag_c * keeping
    real_d = jnp.einsum("mkj,jb->mkb", real_c, cos_two, precision=SPECTRAL) - jnp.einsum(
        "mkj,jb->mkb", imag_c, sin_two, precision=SPECTRAL
    )
    imag_d = jnp.einsum("mkj,jb->mkb", imag_c, cos_two, precision=SPECTRAL) + jnp.einsum(
        "mkj,jb->mkb", real_c, sin_two, precision=SPECTRAL
    )
    real_e = real_d * cos_twist - imag_d * sin_twist
    imag_e = imag_d * cos_twist + real_d * sin_twist
    result = jnp.einsum("mkb,ka->mab", real_e, cos_one, precision=SPECTRAL) - jnp.einsum(
        "mkb,ka->mab", imag_e, sin_one, precision=SPECTRAL
    )
    return (result / length).reshape(row_total, length)


def filter_round(slots, slot_limits):
    slot_total, per_slot, seg_width = slots.shape
    items = slots.reshape(slot_total * per_slot, seg_width)
    whole_rows = lax.all_to_all(items, "lon", split_axis=0, concat_axis=1, tiled=True)
    share = whole_rows.shape[0]
    item_ids = lax.axis_index("lon") * share + jnp.arange(share, dtype=jnp.int32)
    item_limits = jnp.take(slot_limits, item_ids // per_slot)
    filtered = dft_filter(whole_rows, item_limits)
    returned = lax.all_to_all(filtered, "lon", split_axis=1, concat_axis=0, tiled=True)
    return returned.reshape(slot_total, per_slot, seg_width)


def shifted(block, before, after, axis):
    length = block.shape[axis]
    plus = jnp.concatenate([lax.slice_in_dim(block, 1, length, axis=axis), after], axis=axis)
    minus = jnp.concatenate([before, lax.slice_in_dim(block, 0, length - 1, axis=axis)], axis=axis)
    return plus, minus


def on_device(east_wind, north_wind, pressure, sound_squared, column_mass, polar_rows, cutoffs):
    level_count, row_count, seg_width = pressure.shape
    band_count = lax.axis_size("lat")
    band_number = lax.axis_index("lat")
    total_rows = row_count * band_count
    global_rows = band_number * row_count + jnp.arange(row_count, dtype=jnp.int32)
    cosine, courant = latitude_terms(global_rows, total_rows)
    lat_factor = courant[None, :, None]

    p_north, p_south, p_east, p_west = halos(
        pressure[:, 0, :], pressure[:, -1, :], pressure[:, :, 0], pressure[:, :, -1]
    )
    east, west = shifted(pressure, p_west[:, :, None], p_east[:, :, None], 2)
    north, south = shifted(pressure, p_south[:, None, :], p_north[:, None, :], 1)
    east_step = east_wind - lat_factor * (east - west) * 0.5
    north_step = north_wind - 0.3 * (north - south) * 0.5

    slot_count = row_count // 2
    present, choice, limits = slot_table(polar_rows, cutoffs, band_number, row_count, slot_count)
    stacked = jnp.concatenate([east_step, north_step], axis=0)
    picked = jnp.einsum("sr,frc->sfc", choice, stacked, precision=PRECISE)
    whole_limit = seg_width * lax.axis_size("lon") // 2
    smoothed = filter_round(picked, jnp.where(present, limits, whole_limit))
    placed = jnp.einsum("sr,sfc->frc", choice, smoothed, precision=PRECISE)
    listed = jnp.sum(choice, axis=0) > 0.5
    updated = jnp.where(listed[None, :, None], placed, stacked)
    new_east = updated[:level_count]
    new_north = updated[level_count:]

    carried = new_north * cosine[None, :, None]
    v_north, v_south, u_east, u_west = halos(
        carried[:, 0, :], carried[:, -1, :], new_east[:, :, 0], new_east[:, :, -1]
    )
    east_u, west_u = shifted(new_east, u_west[:, :, None], u_east[:, :, None], 2)
    north_v, south_v = shifted(carried, v_south[:, None, :], v_north[:, None, :], 1)
    divergence = (
        lat_factor * (east_u - west_u) * 0.5
        + 0.3 * (north_v - south_v) * 0.5 / cosine[None, :, None]
    )
    new_pressure = pressure - sound_squared[:, None, None] * divergence / column_mass[None]
    return (new_east, new_north, new_pressure)


def solution(mesh):
    in_specs = (
        P(None, "lat", "lon"),
        P(None, "lat", "lon"),
        P(None, "lat", "lon"),
        P(),
        P("lat", "lon"),
        P(),
        P(),
    )
    out_specs = (P(None, "lat", "lon"), P(None, "lat", "lon"), P(None, "lat", "lon"))
    return jax.shard_map(
        on_device, mesh=mesh, in_specs=in_specs, out_specs=out_specs, check_vma=False
    )
```

```python
import jax
import jax.numpy as jnp
from jax import lax
from jax.experimental import pallas as pl
from jax.experimental.pallas import tpu as pltpu
from jax.sharding import PartitionSpec as P

PRECISE = lax.Precision.HIGHEST
SPECTRAL = lax.Precision.HIGH


def shift_pairs(peers, step, wrap):
    pairs = []
    for i in range(peers):
        j = i + step
        if wrap:
            pairs.append((i, j % peers))
        elif 0 <= j < peers:
            pairs.append((i, j))
    return pairs


def halos(lat_first, lat_last, lon_first, lon_last):
    bands = lax.axis_size("lat")
    segs = lax.axis_size("lon")
    north = lax.ppermute(lat_first, "lat", shift_pairs(bands, -1, False))
    south = lax.ppermute(lat_last, "lat", shift_pairs(bands, 1, False))
    east = lax.ppermute(lon_first, "lon", shift_pairs(segs, -1, True))
    west = lax.ppermute(lon_last, "lon", shift_pairs(segs, 1, True))
    return north, south, east, west


def latitude_terms(global_rows, total_rows):
    latitude = (-0.5 + (global_rows.astype(jnp.float32) + 0.5) / total_rows) * jnp.pi
    cosine = jnp.cos(latitude)
    courant = 0.3 * jnp.minimum(1.0 / cosine, 2.0)
    return (cosine, courant)


def slot_table(polar_rows, cutoffs, band_number, row_count, slot_count):
    lower = band_number * row_count
    opening = jnp.sum((polar_rows < lower).astype(jnp.int32))
    closing = jnp.sum((polar_rows < lower + row_count).astype(jnp.int32))
    entries = opening + jnp.arange(slot_count, dtype=jnp.int32)
    present = entries < closing
    safe_entries = jnp.clip(entries, 0, polar_rows.shape[0] - 1)
    local_rows = jnp.take(polar_rows, safe_entries) - lower
    limits = jnp.take(cutoffs, safe_entries)
    rows = jnp.arange(row_count, dtype=jnp.int32)
    choice = ((local_rows[:, None] == rows[None, :]) & present[:, None]).astype(jnp.float32)
    return (present, choice, limits)


def dft_filter(row_data, limits):
    row_total, length = row_data.shape
    inner = 128
    outer = length // inner
    outer_ids = jnp.arange(outer, dtype=jnp.int32)
    inner_ids = jnp.arange(inner, dtype=jnp.int32)
    angle_one = (
        2.0 * jnp.pi * (outer_ids[:, None] * outer_ids[None, :] % outer).astype(jnp.float32) / outer
    )
    angle_two = (
        2.0 * jnp.pi * (inner_ids[:, None] * inner_ids[None, :] % inner).astype(jnp.float32) / inner
    )
    angle_twist = (
        2.0
        * jnp.pi
        * (outer_ids[:, None] * inner_ids[None, :] % length).astype(jnp.float32)
        / length
    )
    cos_one, sin_one = (jnp.cos(angle_one), jnp.sin(angle_one))
    cos_two, sin_two = (jnp.cos(angle_two), jnp.sin(angle_two))
    cos_twist, sin_twist = (jnp.cos(angle_twist), jnp.sin(angle_twist))
    folded = row_data.reshape(row_total, outer, inner)
    real_a = jnp.einsum("mab,ak->mkb", folded, cos_one, precision=SPECTRAL)
    imag_a = -jnp.einsum("mab,ak->mkb", folded, sin_one, precision=SPECTRAL)
    real_b = real_a * cos_twist + imag_a * sin_twist
    imag_b = imag_a * cos_twist - real_a * sin_twist
    real_c = jnp.einsum("mkb,bj->mkj", real_b, cos_two, precision=SPECTRAL) + jnp.einsum(
        "mkb,bj->mkj", imag_b, sin_two, precision=SPECTRAL
    )
    imag_c = jnp.einsum("mkb,bj->mkj", imag_b, cos_two, precision=SPECTRAL) - jnp.einsum(
        "mkb,bj->mkj", real_b, sin_two, precision=SPECTRAL
    )
    wave_ids = outer_ids[:, None] + outer * inner_ids[None, :]
    wave_ids = jnp.minimum(wave_ids, length - wave_ids)
    keeping = (wave_ids[None] <= limits[:, None, None]).astype(jnp.float32)
    real_c = real_c * keeping
    imag_c = imag_c * keeping
    real_d = jnp.einsum("mkj,jb->mkb", real_c, cos_two, precision=SPECTRAL) - jnp.einsum(
        "mkj,jb->mkb", imag_c, sin_two, precision=SPECTRAL
    )
    imag_d = jnp.einsum("mkj,jb->mkb", imag_c, cos_two, precision=SPECTRAL) + jnp.einsum(
        "mkj,jb->mkb", real_c, sin_two, precision=SPECTRAL
    )
    real_e = real_d * cos_twist - imag_d * sin_twist
    imag_e = imag_d * cos_twist + real_d * sin_twist
    result = jnp.einsum("mkb,ka->mab", real_e, cos_one, precision=SPECTRAL) - jnp.einsum(
        "mkb,ka->mab", imag_e, sin_one, precision=SPECTRAL
    )
    return (result / length).reshape(row_total, length)


def filter_round(slots, slot_limits):
    slot_total, per_slot, seg_width = slots.shape
    items = slots.reshape(slot_total * per_slot, seg_width)
    whole_rows = lax.all_to_all(items, "lon", split_axis=0, concat_axis=1, tiled=True)
    share = whole_rows.shape[0]
    item_ids = lax.axis_index("lon") * share + jnp.arange(share, dtype=jnp.int32)
    item_limits = jnp.take(slot_limits, item_ids // per_slot)
    filtered = dft_filter(whole_rows, item_limits)
    returned = lax.all_to_all(filtered, "lon", split_axis=1, concat_axis=0, tiled=True)
    return returned.reshape(slot_total, per_slot, seg_width)


def neighbours(block, before, after, axis):
    length = block.shape[axis]
    places = lax.broadcasted_iota(jnp.int32, block.shape, axis)
    plus = jnp.where(places == length - 1, after, pltpu.roll(block, length - 1, axis))
    minus = jnp.where(places == 0, before, pltpu.roll(block, 1, axis))
    return plus, minus


def step_kernel(cour_ref, ew_ref, nw_ref, p_ref, pn_ref, ps_ref, pe_ref, pw_ref, out_ref):
    p = p_ref[0]
    east, west = neighbours(p, pw_ref[0], pe_ref[0], 1)
    north, south = neighbours(p, ps_ref[0], pn_ref[0], 0)
    out_ref[0, 0] = ew_ref[0] - cour_ref[...] * (east - west) * 0.5
    out_ref[1, 0] = nw_ref[0] - 0.3 * (north - south) * 0.5


def final_kernel(cos_ref, cour_ref, s2_ref, upd_ref, p_ref, mass_ref, vn_ref, vs_ref, ue_ref, uw_ref,
                 ne_ref, nn_ref, np_ref):
    cosv = cos_ref[...]
    u = upd_ref[0, 0]
    v = upd_ref[1, 0]
    ne_ref[0] = u
    nn_ref[0] = v
    carried = v * cosv
    east_u, west_u = neighbours(u, uw_ref[0], ue_ref[0], 1)
    north_v, south_v = neighbours(carried, vs_ref[0], vn_ref[0], 0)
    divergence = (
        cour_ref[...] * (east_u - west_u) * 0.5 + 0.3 * (north_v - south_v) * 0.5 / cosv
    )
    np_ref[0] = p_ref[0] - s2_ref[0] * divergence / mass_ref[...]


def level_spec(rows, width):
    return pl.BlockSpec((1, rows, width), lambda l: (l, 0, 0))


def whole_spec(shape):
    return pl.BlockSpec(shape, lambda l: (0,) * len(shape))


def on_device(east_wind, north_wind, pressure, sound_squared, column_mass, polar_rows, cutoffs):
    level_count, row_count, seg_width = pressure.shape
    band_count = lax.axis_size("lat")
    band_number = lax.axis_index("lat")
    total_rows = row_count * band_count
    global_rows = band_number * row_count + jnp.arange(row_count, dtype=jnp.int32)
    cosine, courant = latitude_terms(global_rows, total_rows)
    cos_col = cosine[:, None]
    cour_col = courant[:, None]
    field = jax.ShapeDtypeStruct((level_count, row_count, seg_width), jnp.float32)
    pair_spec = pl.BlockSpec((2, 1, row_count, seg_width), lambda l: (0, l, 0, 0))

    p_north, p_south, p_east, p_west = halos(
        pressure[:, 0, :], pressure[:, -1, :], pressure[:, :, 0], pressure[:, :, -1]
    )
    steps = pl.pallas_call(
        step_kernel,
        grid=(level_count,),
        in_specs=[
            whole_spec((row_count, 1)),
            level_spec(row_count, seg_width),
            level_spec(row_count, seg_width),
            level_spec(row_count, seg_width),
            level_spec(1, seg_width),
            level_spec(1, seg_width),
            level_spec(row_count, 1),
            level_spec(row_count, 1),
        ],
        out_specs=pair_spec,
        out_shape=jax.ShapeDtypeStruct((2, level_count, row_count, seg_width), jnp.float32),
    )(
        cour_col, east_wind, north_wind, pressure,
        p_north[:, None, :], p_south[:, None, :], p_east[:, :, None], p_west[:, :, None],
    )
    stacked = steps.reshape(2 * level_count, row_count, seg_width)

    slot_count = row_count // 2
    present, choice, limits = slot_table(polar_rows, cutoffs, band_number, row_count, slot_count)
    picked = jnp.einsum("sr,frc->sfc", choice, stacked, precision=PRECISE)
    whole_limit = seg_width * lax.axis_size("lon") // 2
    smoothed = filter_round(picked, jnp.where(present, limits, whole_limit))
    placed = jnp.einsum("sr,sfc->frc", choice, smoothed, precision=PRECISE)
    listed = jnp.sum(choice, axis=0) > 0.5
    updated = jnp.where(listed[None, :, None], placed, stacked)

    v_north, v_south, u_east, u_west = halos(
        updated[level_count:, 0, :] * cosine[0],
        updated[level_count:, -1, :] * cosine[-1],
        updated[:level_count, :, 0],
        updated[:level_count, :, -1],
    )
    return pl.pallas_call(
        final_kernel,
        grid=(level_count,),
        in_specs=[
            whole_spec((row_count, 1)),
            whole_spec((row_count, 1)),
            level_spec(1, 1),
            pair_spec,
            level_spec(row_count, seg_width),
            whole_spec((row_count, seg_width)),
            level_spec(1, seg_width),
            level_spec(1, seg_width),
            level_spec(row_count, 1),
            level_spec(row_count, 1),
        ],
        out_specs=[level_spec(row_count, seg_width)] * 3,
        out_shape=[field] * 3,
    )(
        cos_col, cour_col, sound_squared[:, None, None],
        updated.reshape(2, level_count, row_count, seg_width), pressure, column_mass,
        v_north[:, None, :], v_south[:, None, :], u_east[:, :, None], u_west[:, :, None],
    )


def solution(mesh):
    in_specs = (
        P(None, "lat", "lon"),
        P(None, "lat", "lon"),
        P(None, "lat", "lon"),
        P(),
        P("lat", "lon"),
        P(),
        P(),
    )
    out_specs = (P(None, "lat", "lon"), P(None, "lat", "lon"), P(None, "lat", "lon"))
    return jax.shard_map(
        on_device, mesh=mesh, in_specs=in_specs, out_specs=out_specs, check_vma=False
    )
```

```python
import jax
import jax.numpy as jnp
from jax import lax
from jax.sharding import PartitionSpec as P

PRECISE = lax.Precision.HIGHEST
SPECTRAL = lax.Precision.HIGH


def shift_pairs(peers, step, wrap):
    pairs = []
    for i in range(peers):
        j = i + step
        if wrap:
            pairs.append((i, j % peers))
        elif 0 <= j < peers:
            pairs.append((i, j))
    return pairs


def halos(lat_first, lat_last, lon_first, lon_last):
    bands = lax.axis_size("lat")
    segs = lax.axis_size("lon")
    north = lax.ppermute(lat_first, "lat", shift_pairs(bands, -1, False))
    south = lax.ppermute(lat_last, "lat", shift_pairs(bands, 1, False))
    east = lax.ppermute(lon_first, "lon", shift_pairs(segs, -1, True))
    west = lax.ppermute(lon_last, "lon", shift_pairs(segs, 1, True))
    return north, south, east, west


def latitude_terms(global_rows, total_rows):
    latitude = (-0.5 + (global_rows.astype(jnp.float32) + 0.5) / total_rows) * jnp.pi
    cosine = jnp.cos(latitude)
    courant = 0.3 * jnp.minimum(1.0 / cosine, 2.0)
    return (cosine, courant)


def slot_table(polar_rows, cutoffs, band_number, row_count, slot_count):
    lower = band_number * row_count
    opening = jnp.sum((polar_rows < lower).astype(jnp.int32))
    closing = jnp.sum((polar_rows < lower + row_count).astype(jnp.int32))
    entries = opening + jnp.arange(slot_count, dtype=jnp.int32)
    present = entries < closing
    safe_entries = jnp.clip(entries, 0, polar_rows.shape[0] - 1)
    local_rows = jnp.take(polar_rows, safe_entries) - lower
    limits = jnp.take(cutoffs, safe_entries)
    rows = jnp.arange(row_count, dtype=jnp.int32)
    choice = ((local_rows[:, None] == rows[None, :]) & present[:, None]).astype(jnp.float32)
    return (present, choice, limits)


def dft_filter(pieces, limits):
    piece_count, row_total, width = pieces.shape
    length = piece_count * width
    inner = 128
    split = width // inner
    outer = length // inner
    outer_ids = jnp.arange(outer, dtype=jnp.int32)
    inner_ids = jnp.arange(inner, dtype=jnp.int32)
    angle_one = (
        2.0 * jnp.pi * (outer_ids[:, None] * outer_ids[None, :] % outer).astype(jnp.float32) / outer
    )
    angle_two = (
        2.0 * jnp.pi * (inner_ids[:, None] * inner_ids[None, :] % inner).astype(jnp.float32) / inner
    )
    angle_twist = (
        2.0
        * jnp.pi
        * (outer_ids[:, None] * inner_ids[None, :] % length).astype(jnp.float32)
        / length
    )
    cos_one, sin_one = (jnp.cos(angle_one), jnp.sin(angle_one))
    cos_two, sin_two = (jnp.cos(angle_two), jnp.sin(angle_two))
    cos_twist = jnp.cos(angle_twist)[:, None, :]
    sin_twist = jnp.sin(angle_twist)[:, None, :]
    real_a = 0.0
    imag_a = 0.0
    for part in range(split):
        block = pieces[:, :, part * inner:(part + 1) * inner]
        real_a = real_a + jnp.einsum(
            "sqb,sk->kqb", block, cos_one[part::split], precision=SPECTRAL
        )
        imag_a = imag_a - jnp.einsum(
            "sqb,sk->kqb", block, sin_one[part::split], precision=SPECTRAL
        )
    real_b = real_a * cos_twist + imag_a * sin_twist
    imag_b = imag_a * cos_twist - real_a * sin_twist
    real_c = jnp.einsum("kqb,bj->kqj", real_b, cos_two, precision=SPECTRAL) + jnp.einsum(
        "kqb,bj->kqj", imag_b, sin_two, precision=SPECTRAL
    )
    imag_c = jnp.einsum("kqb,bj->kqj", imag_b, cos_two, precision=SPECTRAL) - jnp.einsum(
        "kqb,bj->kqj", real_b, sin_two, precision=SPECTRAL
    )
    wave_ids = outer_ids[:, None] + outer * inner_ids[None, :]
    wave_ids = jnp.minimum(wave_ids, length - wave_ids)
    keeping = (wave_ids[:, None, :] <= limits[None, :, None]).astype(jnp.float32)
    real_c = real_c * keeping
    imag_c = imag_c * keeping
    real_d = jnp.einsum("kqj,jb->kqb", real_c, cos_two, precision=SPECTRAL) - jnp.einsum(
        "kqj,jb->kqb", imag_c, sin_two, precision=SPECTRAL
    )
    imag_d = jnp.einsum("kqj,jb->kqb", imag_c, cos_two, precision=SPECTRAL) + jnp.einsum(
        "kqj,jb->kqb", real_c, sin_two, precision=SPECTRAL
    )
    real_e = real_d * cos_twist - imag_d * sin_twist
    imag_e = imag_d * cos_twist + real_d * sin_twist
    parts = []
    for part in range(split):
        parts.append(
            jnp.einsum("kqb,ks->sqb", real_e, cos_one[:, part::split], precision=SPECTRAL)
            - jnp.einsum("kqb,ks->sqb", imag_e, sin_one[:, part::split], precision=SPECTRAL)
        )
    return jnp.concatenate(parts, axis=2) / length


def filter_round(slots, slot_limits):
    slot_total, per_slot, seg_width = slots.shape
    peers = lax.axis_size("lon")
    items = slots.reshape(peers, slot_total * per_slot // peers, seg_width)
    pieces = lax.all_to_all(items, "lon", split_axis=0, concat_axis=0, tiled=True)
    share = pieces.shape[1]
    item_ids = lax.axis_index("lon") * share + jnp.arange(share, dtype=jnp.int32)
    item_limits = jnp.take(slot_limits, item_ids // per_slot)
    filtered = dft_filter(pieces, item_limits)
    returned = lax.all_to_all(filtered, "lon", split_axis=0, concat_axis=0, tiled=True)
    return returned.reshape(slot_total, per_slot, seg_width)


def shifted(block, before, after, axis):
    length = block.shape[axis]
    plus = jnp.concatenate([lax.slice_in_dim(block, 1, length, axis=axis), after], axis=axis)
    minus = jnp.concatenate([before, lax.slice_in_dim(block, 0, length - 1, axis=axis)], axis=axis)
    return plus, minus


def on_device(east_wind, north_wind, pressure, sound_squared, column_mass, polar_rows, cutoffs):
    level_count, row_count, seg_width = pressure.shape
    band_count = lax.axis_size("lat")
    band_number = lax.axis_index("lat")
    total_rows = row_count * band_count
    global_rows = band_number * row_count + jnp.arange(row_count, dtype=jnp.int32)
    cosine, courant = latitude_terms(global_rows, total_rows)
    lat_factor = courant[None, :, None]

    p_north, p_south, p_east, p_west = halos(
        pressure[:, 0, :], pressure[:, -1, :], pressure[:, :, 0], pressure[:, :, -1]
    )
    east, west = shifted(pressure, p_west[:, :, None], p_east[:, :, None], 2)
    north, south = shifted(pressure, p_south[:, None, :], p_north[:, None, :], 1)
    east_step = east_wind - lat_factor * (east - west) * 0.5
    north_step = north_wind - 0.3 * (north - south) * 0.5

    slot_count = row_count // 2
    present, choice, limits = slot_table(polar_rows, cutoffs, band_number, row_count, slot_count)
    stacked = jnp.concatenate([east_step, north_step], axis=0)
    picked = jnp.einsum("sr,frc->sfc", choice, stacked, precision=PRECISE)
    whole_limit = seg_width * lax.axis_size("lon") // 2
    smoothed = filter_round(picked, jnp.where(present, limits, whole_limit))
    placed = jnp.einsum("sr,sfc->frc", choice, smoothed, precision=PRECISE)
    listed = jnp.sum(choice, axis=0) > 0.5
    updated = jnp.where(listed[None, :, None], placed, stacked)
    new_east = updated[:level_count]
    new_north = updated[level_count:]

    carried = new_north * cosine[None, :, None]
    v_north, v_south, u_east, u_west = halos(
        carried[:, 0, :], carried[:, -1, :], new_east[:, :, 0], new_east[:, :, -1]
    )
    east_u, west_u = shifted(new_east, u_west[:, :, None], u_east[:, :, None], 2)
    north_v, south_v = shifted(carried, v_south[:, None, :], v_north[:, None, :], 1)
    divergence = (
        lat_factor * (east_u - west_u) * 0.5
        + 0.3 * (north_v - south_v) * 0.5 / cosine[None, :, None]
    )
    new_pressure = pressure - sound_squared[:, None, None] * divergence / column_mass[None]
    return (new_east, new_north, new_pressure)


def solution(mesh):
    in_specs = (
        P(None, "lat", "lon"),
        P(None, "lat", "lon"),
        P(None, "lat", "lon"),
        P(),
        P("lat", "lon"),
        P(),
        P(),
    )
    out_specs = (P(None, "lat", "lon"), P(None, "lat", "lon"), P(None, "lat", "lon"))
    return jax.shard_map(
        on_device, mesh=mesh, in_specs=in_specs, out_specs=out_specs, check_vma=False
    )
```

```python
import jax
import jax.numpy as jnp
from jax import lax
from jax.sharding import PartitionSpec as P

PRECISE = lax.Precision.HIGHEST
SPECTRAL = lax.Precision.HIGH


def shift_pairs(peers, step, wrap):
    pairs = []
    for i in range(peers):
        j = i + step
        if wrap:
            pairs.append((i, j % peers))
        elif 0 <= j < peers:
            pairs.append((i, j))
    return pairs


def halos(lat_first, lat_last, lon_first, lon_last):
    bands = lax.axis_size("lat")
    segs = lax.axis_size("lon")
    north = lax.ppermute(lat_first, "lat", shift_pairs(bands, -1, False))
    south = lax.ppermute(lat_last, "lat", shift_pairs(bands, 1, False))
    east = lax.ppermute(lon_first, "lon", shift_pairs(segs, -1, True))
    west = lax.ppermute(lon_last, "lon", shift_pairs(segs, 1, True))
    return north, south, east, west


def latitude_terms(global_rows, total_rows):
    latitude = (-0.5 + (global_rows.astype(jnp.float32) + 0.5) / total_rows) * jnp.pi
    cosine = jnp.cos(latitude)
    courant = 0.3 * jnp.minimum(1.0 / cosine, 2.0)
    return (cosine, courant)


def slot_table(polar_rows, cutoffs, band_number, row_count, slot_count):
    lower = band_number * row_count
    opening = jnp.sum((polar_rows < lower).astype(jnp.int32))
    closing = jnp.sum((polar_rows < lower + row_count).astype(jnp.int32))
    entries = opening + jnp.arange(slot_count, dtype=jnp.int32)
    present = entries < closing
    safe_entries = jnp.clip(entries, 0, polar_rows.shape[0] - 1)
    local_rows = jnp.take(polar_rows, safe_entries) - lower
    limits = jnp.take(cutoffs, safe_entries)
    rows = jnp.arange(row_count, dtype=jnp.int32)
    choice = ((local_rows[:, None] == rows[None, :]) & present[:, None]).astype(jnp.float32)
    return (present, choice, limits)


def dft_filter(pieces, limits):
    piece_count, row_total, width = pieces.shape
    length = piece_count * width
    inner = 128
    split = width // inner
    outer = length // inner
    outer_ids = jnp.arange(outer, dtype=jnp.int32)
    inner_ids = jnp.arange(inner, dtype=jnp.int32)
    angle_one = (
        2.0 * jnp.pi * (outer_ids[:, None] * outer_ids[None, :] % outer).astype(jnp.float32) / outer
    )
    angle_two = (
        2.0 * jnp.pi * (inner_ids[:, None] * inner_ids[None, :] % inner).astype(jnp.float32) / inner
    )
    angle_twist = (
        2.0
        * jnp.pi
        * (outer_ids[:, None] * inner_ids[None, :] % length).astype(jnp.float32)
        / length
    )
    cos_one, sin_one = (jnp.cos(angle_one), jnp.sin(angle_one))
    cos_two, sin_two = (jnp.cos(angle_two), jnp.sin(angle_two))
    cos_twist = jnp.cos(angle_twist)[:, None, :]
    sin_twist = jnp.sin(angle_twist)[:, None, :]
    first = jnp.concatenate([cos_one, -sin_one], axis=1)
    forward = jnp.concatenate(
        [jnp.concatenate([cos_two, -sin_two], axis=1), jnp.concatenate([sin_two, cos_two], axis=1)],
        axis=0,
    )
    backward = jnp.concatenate(
        [jnp.concatenate([cos_two, sin_two], axis=1), jnp.concatenate([-sin_two, cos_two], axis=1)],
        axis=0,
    )
    last = jnp.concatenate([cos_one, -sin_one], axis=0)
    spectrum = 0.0
    for part in range(split):
        block = pieces[:, :, part * inner:(part + 1) * inner]
        spectrum = spectrum + jnp.einsum(
            "sqb,sk->kqb", block, first[part::split], precision=SPECTRAL
        )
    real_a = spectrum[:outer]
    imag_a = spectrum[outer:]
    real_b = real_a * cos_twist + imag_a * sin_twist
    imag_b = imag_a * cos_twist - real_a * sin_twist
    mixed = jnp.einsum(
        "kqb,bj->kqj", jnp.concatenate([real_b, imag_b], axis=2), forward, precision=SPECTRAL
    )
    wave_ids = outer_ids[:, None] + outer * inner_ids[None, :]
    wave_ids = jnp.minimum(wave_ids, length - wave_ids)
    keeping = (wave_ids[:, None, :] <= limits[None, :, None]).astype(jnp.float32)
    mixed = mixed * jnp.concatenate([keeping, keeping], axis=2)
    back = jnp.einsum("kqj,jb->kqb", mixed, backward, precision=SPECTRAL)
    real_d = back[:, :, :inner]
    imag_d = back[:, :, inner:]
    real_e = real_d * cos_twist - imag_d * sin_twist
    imag_e = imag_d * cos_twist + real_d * sin_twist
    stacked = jnp.concatenate([real_e, imag_e], axis=0)
    parts = []
    for part in range(split):
        parts.append(
            jnp.einsum("kqb,ks->sqb", stacked, last[:, part::split], precision=SPECTRAL)
        )
    return jnp.concatenate(parts, axis=2) / length


def filter_round(slots, slot_limits):
    field_count, slot_total, seg_width = slots.shape
    peers = lax.axis_size("lon")
    items = slots.reshape(peers, field_count * slot_total // peers, seg_width)
    pieces = lax.all_to_all(items, "lon", split_axis=0, concat_axis=0, tiled=True)
    share = pieces.shape[1]
    item_ids = lax.axis_index("lon") * share + jnp.arange(share, dtype=jnp.int32)
    item_limits = jnp.take(slot_limits, item_ids % slot_total)
    filtered = dft_filter(pieces, item_limits)
    returned = lax.all_to_all(filtered, "lon", split_axis=0, concat_axis=0, tiled=True)
    return returned.reshape(field_count, slot_total, seg_width)


def shifted(block, before, after, axis):
    length = block.shape[axis]
    plus = jnp.concatenate([lax.slice_in_dim(block, 1, length, axis=axis), after], axis=axis)
    minus = jnp.concatenate([before, lax.slice_in_dim(block, 0, length - 1, axis=axis)], axis=axis)
    return plus, minus


def on_device(east_wind, north_wind, pressure, sound_squared, column_mass, polar_rows, cutoffs):
    level_count, row_count, seg_width = pressure.shape
    band_count = lax.axis_size("lat")
    band_number = lax.axis_index("lat")
    total_rows = row_count * band_count
    global_rows = band_number * row_count + jnp.arange(row_count, dtype=jnp.int32)
    cosine, courant = latitude_terms(global_rows, total_rows)
    lat_factor = courant[None, :, None]

    p_north, p_south, p_east, p_west = halos(
        pressure[:, 0, :], pressure[:, -1, :], pressure[:, :, 0], pressure[:, :, -1]
    )
    east, west = shifted(pressure, p_west[:, :, None], p_east[:, :, None], 2)
    north, south = shifted(pressure, p_south[:, None, :], p_north[:, None, :], 1)
    east_step = east_wind - lat_factor * (east - west) * 0.5
    north_step = north_wind - 0.3 * (north - south) * 0.5

    slot_count = row_count // 2
    present, choice, limits = slot_table(polar_rows, cutoffs, band_number, row_count, slot_count)
    stacked = jnp.concatenate([east_step, north_step], axis=0)
    picked = jnp.einsum("sr,frc->fsc", choice, stacked, precision=PRECISE)
    whole_limit = seg_width * lax.axis_size("lon") // 2
    smoothed = filter_round(picked, jnp.where(present, limits, whole_limit))
    placed = jnp.einsum("sr,fsc->frc", choice, smoothed, precision=PRECISE)
    listed = jnp.sum(choice, axis=0) > 0.5
    updated = jnp.where(listed[None, :, None], placed, stacked)
    new_east = updated[:level_count]
    new_north = updated[level_count:]

    carried = new_north * cosine[None, :, None]
    v_north, v_south, u_east, u_west = halos(
        carried[:, 0, :], carried[:, -1, :], new_east[:, :, 0], new_east[:, :, -1]
    )
    east_u, west_u = shifted(new_east, u_west[:, :, None], u_east[:, :, None], 2)
    north_v, south_v = shifted(carried, v_south[:, None, :], v_north[:, None, :], 1)
    divergence = (
        lat_factor * (east_u - west_u) * 0.5
        + 0.3 * (north_v - south_v) * 0.5 / cosine[None, :, None]
    )
    new_pressure = pressure - sound_squared[:, None, None] * divergence / column_mass[None]
    return (new_east, new_north, new_pressure)


def solution(mesh):
    in_specs = (
        P(None, "lat", "lon"),
        P(None, "lat", "lon"),
        P(None, "lat", "lon"),
        P(),
        P("lat", "lon"),
        P(),
        P(),
    )
    out_specs = (P(None, "lat", "lon"), P(None, "lat", "lon"), P(None, "lat", "lon"))
    return jax.shard_map(
        on_device, mesh=mesh, in_specs=in_specs, out_specs=out_specs, check_vma=False
    )
```

```python
import jax
import jax.numpy as jnp
from jax import lax
from jax.sharding import PartitionSpec as P

PRECISE = lax.Precision.HIGHEST
SPECTRAL = lax.Precision.HIGH


def shift_pairs(peers, step, wrap):
    pairs = []
    for i in range(peers):
        j = i + step
        if wrap:
            pairs.append((i, j % peers))
        elif 0 <= j < peers:
            pairs.append((i, j))
    return pairs


def halos(lat_first, lat_last, lon_first, lon_last):
    bands = lax.axis_size("lat")
    segs = lax.axis_size("lon")
    north = lax.ppermute(lat_first, "lat", shift_pairs(bands, -1, False))
    south = lax.ppermute(lat_last, "lat", shift_pairs(bands, 1, False))
    east = lax.ppermute(lon_first, "lon", shift_pairs(segs, -1, True))
    west = lax.ppermute(lon_last, "lon", shift_pairs(segs, 1, True))
    return north, south, east, west


def latitude_terms(global_rows, total_rows):
    latitude = (-0.5 + (global_rows.astype(jnp.float32) + 0.5) / total_rows) * jnp.pi
    cosine = jnp.cos(latitude)
    courant = 0.3 * jnp.minimum(1.0 / cosine, 2.0)
    return (cosine, courant)


def slot_table(polar_rows, cutoffs, band_number, row_count, slot_count):
    lower = band_number * row_count
    opening = jnp.sum((polar_rows < lower).astype(jnp.int32))
    spare = jnp.full((slot_count,), -1, jnp.int32)
    entries = lax.dynamic_slice(jnp.concatenate([polar_rows, spare]), (opening,), (slot_count,))
    limits = lax.dynamic_slice(jnp.concatenate([cutoffs, spare]), (opening,), (slot_count,))
    local_rows = entries - lower
    present = (local_rows >= 0) & (local_rows < row_count)
    rows = jnp.arange(row_count, dtype=jnp.int32)
    choice = (local_rows[:, None] == rows[None, :]).astype(jnp.float32)
    return (present, choice, limits)


def dft_filter(pieces, limits):
    piece_count, row_total, width = pieces.shape
    length = piece_count * width
    inner = 128
    split = width // inner
    outer = length // inner
    outer_ids = jnp.arange(outer, dtype=jnp.int32)
    inner_ids = jnp.arange(inner, dtype=jnp.int32)
    angle_one = (
        2.0 * jnp.pi * (outer_ids[:, None] * outer_ids[None, :] % outer).astype(jnp.float32) / outer
    )
    angle_two = (
        2.0 * jnp.pi * (inner_ids[:, None] * inner_ids[None, :] % inner).astype(jnp.float32) / inner
    )
    angle_twist = (
        2.0
        * jnp.pi
        * (outer_ids[:, None] * inner_ids[None, :] % length).astype(jnp.float32)
        / length
    )
    cos_one, sin_one = (jnp.cos(angle_one), jnp.sin(angle_one))
    cos_two, sin_two = (jnp.cos(angle_two), jnp.sin(angle_two))
    cos_twist = jnp.cos(angle_twist)[:, None, :]
    sin_twist = jnp.sin(angle_twist)[:, None, :]
    first = jnp.concatenate([cos_one, -sin_one], axis=1)
    forward = jnp.concatenate(
        [jnp.concatenate([cos_two, -sin_two], axis=1), jnp.concatenate([sin_two, cos_two], axis=1)],
        axis=0,
    )
    backward = jnp.concatenate(
        [jnp.concatenate([cos_two, sin_two], axis=1), jnp.concatenate([-sin_two, cos_two], axis=1)],
        axis=0,
    )
    last = jnp.concatenate([cos_one, -sin_one], axis=0)
    spectrum = 0.0
    for part in range(split):
        block = pieces[:, :, part * inner:(part + 1) * inner]
        spectrum = spectrum + jnp.einsum(
            "sqb,sk->kqb", block, first[part::split], precision=SPECTRAL
        )
    real_a = spectrum[:outer]
    imag_a = spectrum[outer:]
    real_b = real_a * cos_twist + imag_a * sin_twist
    imag_b = imag_a * cos_twist - real_a * sin_twist
    mixed = jnp.einsum(
        "kqb,bj->kqj", jnp.concatenate([real_b, imag_b], axis=2), forward, precision=SPECTRAL
    )
    wave_ids = outer_ids[:, None] + outer * inner_ids[None, :]
    wave_ids = jnp.minimum(wave_ids, length - wave_ids)
    keeping = (wave_ids[:, None, :] <= limits[None, :, None]).astype(jnp.float32)
    mixed = mixed * jnp.concatenate([keeping, keeping], axis=2)
    back = jnp.einsum("kqj,jb->kqb", mixed, backward, precision=SPECTRAL)
    real_d = back[:, :, :inner]
    imag_d = back[:, :, inner:]
    real_e = real_d * cos_twist - imag_d * sin_twist
    imag_e = imag_d * cos_twist + real_d * sin_twist
    stacked = jnp.concatenate([real_e, imag_e], axis=0)
    parts = []
    for part in range(split):
        parts.append(
            jnp.einsum("kqb,ks->sqb", stacked, last[:, part::split], precision=SPECTRAL)
        )
    return jnp.concatenate(parts, axis=2) / length


def filter_round(slots, slot_limits):
    field_count, slot_total, seg_width = slots.shape
    peers = lax.axis_size("lon")
    items = slots.reshape(peers, field_count * slot_total // peers, seg_width)
    pieces = lax.all_to_all(items, "lon", split_axis=0, concat_axis=0, tiled=True)
    share = pieces.shape[1]
    item_ids = lax.axis_index("lon") * share + jnp.arange(share, dtype=jnp.int32)
    item_limits = jnp.take(slot_limits, item_ids % slot_total)
    filtered = dft_filter(pieces, item_limits)
    returned = lax.all_to_all(filtered, "lon", split_axis=0, concat_axis=0, tiled=True)
    return returned.reshape(field_count, slot_total, seg_width)


def shifted(block, before, after, axis):
    length = block.shape[axis]
    plus = jnp.concatenate([lax.slice_in_dim(block, 1, length, axis=axis), after], axis=axis)
    minus = jnp.concatenate([before, lax.slice_in_dim(block, 0, length - 1, axis=axis)], axis=axis)
    return plus, minus


def on_device(east_wind, north_wind, pressure, sound_squared, column_mass, polar_rows, cutoffs):
    level_count, row_count, seg_width = pressure.shape
    band_count = lax.axis_size("lat")
    band_number = lax.axis_index("lat")
    total_rows = row_count * band_count
    global_rows = band_number * row_count + jnp.arange(row_count, dtype=jnp.int32)
    cosine, courant = latitude_terms(global_rows, total_rows)
    lat_factor = courant[None, :, None]

    p_north, p_south, p_east, p_west = halos(
        pressure[:, 0, :], pressure[:, -1, :], pressure[:, :, 0], pressure[:, :, -1]
    )
    east, west = shifted(pressure, p_west[:, :, None], p_east[:, :, None], 2)
    north, south = shifted(pressure, p_south[:, None, :], p_north[:, None, :], 1)
    east_step = east_wind - lat_factor * (east - west) * 0.5
    north_step = north_wind - 0.3 * (north - south) * 0.5

    slot_count = row_count // 2
    present, choice, limits = slot_table(polar_rows, cutoffs, band_number, row_count, slot_count)
    stacked = jnp.concatenate([east_step, north_step], axis=0)
    picked = jnp.einsum("sr,frc->fsc", choice, stacked, precision=PRECISE)
    whole_limit = seg_width * lax.axis_size("lon") // 2
    smoothed = filter_round(picked, jnp.where(present, limits, whole_limit))
    placed = jnp.einsum("sr,fsc->frc", choice, smoothed, precision=PRECISE)
    listed = jnp.sum(choice, axis=0) > 0.5
    updated = jnp.where(listed[None, :, None], placed, stacked)
    new_east = updated[:level_count]
    new_north = updated[level_count:]

    carried = new_north * cosine[None, :, None]
    v_north, v_south, u_east, u_west = halos(
        carried[:, 0, :], carried[:, -1, :], new_east[:, :, 0], new_east[:, :, -1]
    )
    east_u, west_u = shifted(new_east, u_west[:, :, None], u_east[:, :, None], 2)
    north_v, south_v = shifted(carried, v_south[:, None, :], v_north[:, None, :], 1)
    divergence = (
        lat_factor * (east_u - west_u) * 0.5
        + 0.3 * (north_v - south_v) * 0.5 / cosine[None, :, None]
    )
    new_pressure = pressure - sound_squared[:, None, None] * divergence / column_mass[None]
    return (new_east, new_north, new_pressure)


def solution(mesh):
    in_specs = (
        P(None, "lat", "lon"),
        P(None, "lat", "lon"),
        P(None, "lat", "lon"),
        P(),
        P("lat", "lon"),
        P(),
        P(),
    )
    out_specs = (P(None, "lat", "lon"), P(None, "lat", "lon"), P(None, "lat", "lon"))
    return jax.shard_map(
        on_device, mesh=mesh, in_specs=in_specs, out_specs=out_specs, check_vma=False
    )
```

```python
import jax
import jax.numpy as jnp
from jax import lax
from jax.sharding import PartitionSpec as P

PRECISE = lax.Precision.HIGHEST
SPECTRAL = lax.Precision.HIGH


def shift_pairs(peers, step, wrap):
    pairs = []
    for i in range(peers):
        j = i + step
        if wrap:
            pairs.append((i, j % peers))
        elif 0 <= j < peers:
            pairs.append((i, j))
    return pairs


def halos(lat_first, lat_last, lon_first, lon_last):
    bands = lax.axis_size("lat")
    segs = lax.axis_size("lon")
    north = lax.ppermute(lat_first, "lat", shift_pairs(bands, -1, False))
    south = lax.ppermute(lat_last, "lat", shift_pairs(bands, 1, False))
    east = lax.ppermute(lon_first, "lon", shift_pairs(segs, -1, True))
    west = lax.ppermute(lon_last, "lon", shift_pairs(segs, 1, True))
    return north, south, east, west


def latitude_terms(global_rows, total_rows):
    latitude = (-0.5 + (global_rows.astype(jnp.float32) + 0.5) / total_rows) * jnp.pi
    cosine = jnp.cos(latitude)
    courant = 0.3 * jnp.minimum(1.0 / cosine, 2.0)
    return (cosine, courant)


def slot_table(polar_rows, cutoffs, band_number, row_count, slot_count):
    lower = band_number * row_count
    opening = jnp.sum((polar_rows < lower).astype(jnp.int32))
    spare = jnp.full((slot_count,), -1, jnp.int32)
    entries = lax.dynamic_slice(jnp.concatenate([polar_rows, spare]), (opening,), (slot_count,))
    limits = lax.dynamic_slice(jnp.concatenate([cutoffs, spare]), (opening,), (slot_count,))
    local_rows = entries - lower
    present = (local_rows >= 0) & (local_rows < row_count)
    rows = jnp.arange(row_count, dtype=jnp.int32)
    choice = (local_rows[:, None] == rows[None, :]).astype(jnp.float32)
    return (present, choice, limits, local_rows)


def dft_filter(pieces, limits):
    piece_count, row_total, width = pieces.shape
    length = piece_count * width
    inner = 128
    split = width // inner
    outer = length // inner
    outer_ids = jnp.arange(outer, dtype=jnp.int32)
    inner_ids = jnp.arange(inner, dtype=jnp.int32)
    angle_one = (
        2.0 * jnp.pi * (outer_ids[:, None] * outer_ids[None, :] % outer).astype(jnp.float32) / outer
    )
    angle_two = (
        2.0 * jnp.pi * (inner_ids[:, None] * inner_ids[None, :] % inner).astype(jnp.float32) / inner
    )
    angle_twist = (
        2.0
        * jnp.pi
        * (outer_ids[:, None] * inner_ids[None, :] % length).astype(jnp.float32)
        / length
    )
    cos_one, sin_one = (jnp.cos(angle_one), jnp.sin(angle_one))
    cos_two, sin_two = (jnp.cos(angle_two), jnp.sin(angle_two))
    cos_twist = jnp.cos(angle_twist)[:, None, :]
    sin_twist = jnp.sin(angle_twist)[:, None, :]
    first = jnp.concatenate([cos_one, -sin_one], axis=1)
    forward = jnp.concatenate(
        [jnp.concatenate([cos_two, -sin_two], axis=1), jnp.concatenate([sin_two, cos_two], axis=1)],
        axis=0,
    )
    backward = jnp.concatenate(
        [jnp.concatenate([cos_two, sin_two], axis=1), jnp.concatenate([-sin_two, cos_two], axis=1)],
        axis=0,
    )
    last = jnp.concatenate([cos_one, -sin_one], axis=0)
    spectrum = 0.0
    for part in range(split):
        block = pieces[:, :, part * inner:(part + 1) * inner]
        spectrum = spectrum + jnp.einsum(
            "sqb,sk->kqb", block, first[part::split], precision=SPECTRAL
        )
    real_a = spectrum[:outer]
    imag_a = spectrum[outer:]
    real_b = real_a * cos_twist + imag_a * sin_twist
    imag_b = imag_a * cos_twist - real_a * sin_twist
    mixed = jnp.einsum(
        "kqb,bj->kqj", jnp.concatenate([real_b, imag_b], axis=2), forward, precision=SPECTRAL
    )
    wave_ids = outer_ids[:, None] + outer * inner_ids[None, :]
    wave_ids = jnp.minimum(wave_ids, length - wave_ids)
    keeping = (wave_ids[:, None, :] <= limits[None, :, None]).astype(jnp.float32)
    mixed = mixed * jnp.concatenate([keeping, keeping], axis=2)
    back = jnp.einsum("kqj,jb->kqb", mixed, backward, precision=SPECTRAL)
    real_d = back[:, :, :inner]
    imag_d = back[:, :, inner:]
    real_e = real_d * cos_twist - imag_d * sin_twist
    imag_e = imag_d * cos_twist + real_d * sin_twist
    stacked = jnp.concatenate([real_e, imag_e], axis=0)
    parts = []
    for part in range(split):
        parts.append(
            jnp.einsum("kqb,ks->sqb", stacked, last[:, part::split], precision=SPECTRAL)
        )
    return jnp.concatenate(parts, axis=2) / length


def filter_round(slots, slot_limits):
    field_count, slot_total, seg_width = slots.shape
    peers = lax.axis_size("lon")
    items = slots.reshape(peers, field_count * slot_total // peers, seg_width)
    pieces = lax.all_to_all(items, "lon", split_axis=0, concat_axis=0, tiled=True)
    share = pieces.shape[1]
    item_ids = lax.axis_index("lon") * share + jnp.arange(share, dtype=jnp.int32)
    item_limits = jnp.take(slot_limits, item_ids % slot_total)
    filtered = dft_filter(pieces, item_limits)
    returned = lax.all_to_all(filtered, "lon", split_axis=0, concat_axis=0, tiled=True)
    return returned.reshape(field_count, slot_total, seg_width)


def shifted(block, before, after, axis):
    length = block.shape[axis]
    plus = jnp.concatenate([lax.slice_in_dim(block, 1, length, axis=axis), after], axis=axis)
    minus = jnp.concatenate([before, lax.slice_in_dim(block, 0, length - 1, axis=axis)], axis=axis)
    return plus, minus


def on_device(east_wind, north_wind, pressure, sound_squared, column_mass, polar_rows, cutoffs):
    level_count, row_count, seg_width = pressure.shape
    band_count = lax.axis_size("lat")
    band_number = lax.axis_index("lat")
    total_rows = row_count * band_count
    global_rows = band_number * row_count + jnp.arange(row_count, dtype=jnp.int32)
    cosine, courant = latitude_terms(global_rows, total_rows)
    lat_factor = courant[None, :, None]

    p_north, p_south, p_east, p_west = halos(
        pressure[:, 0, :], pressure[:, -1, :], pressure[:, :, 0], pressure[:, :, -1]
    )
    east, west = shifted(pressure, p_west[:, :, None], p_east[:, :, None], 2)
    north, south = shifted(pressure, p_south[:, None, :], p_north[:, None, :], 1)
    east_step = east_wind - lat_factor * (east - west) * 0.5
    north_step = north_wind - 0.3 * (north - south) * 0.5

    slot_count = row_count // 2
    present, choice, limits, local_rows = slot_table(
        polar_rows, cutoffs, band_number, row_count, slot_count
    )
    rows = jnp.arange(row_count, dtype=jnp.int32)
    above = (local_rows[:, None] + 1 == rows[None, :]).astype(jnp.float32)
    below = (local_rows[:, None] - 1 == rows[None, :]).astype(jnp.float32)
    top = (local_rows == row_count - 1)[None, :, None]
    bottom = (local_rows == 0)[None, :, None]

    def gather(weights, block):
        return jnp.einsum("sr,lrc->lsc", weights, block, precision=PRECISE)

    p_rows = gather(choice, pressure)
    pe_rows = jnp.einsum("sr,lr->ls", choice, p_east, precision=PRECISE)
    pw_rows = jnp.einsum("sr,lr->ls", choice, p_west, precision=PRECISE)
    cour_rows = jnp.einsum("sr,r->s", choice, courant, precision=PRECISE)
    pn_rows = gather(above, pressure) + jnp.where(top, p_north[:, None, :], 0.0)
    ps_rows = gather(below, pressure) + jnp.where(bottom, p_south[:, None, :], 0.0)
    east_r, west_r = shifted(p_rows, pw_rows[:, :, None], pe_rows[:, :, None], 2)
    east_rows = gather(choice, east_wind) - cour_rows[None, :, None] * (east_r - west_r) * 0.5
    north_rows = gather(choice, north_wind) - 0.3 * (pn_rows - ps_rows) * 0.5
    picked = jnp.concatenate([east_rows, north_rows], axis=0)
    stacked = jnp.concatenate([east_step, north_step], axis=0)
    whole_limit = seg_width * lax.axis_size("lon") // 2
    smoothed = filter_round(picked, jnp.where(present, limits, whole_limit))
    placed = jnp.einsum("sr,fsc->frc", choice, smoothed, precision=PRECISE)
    listed = jnp.sum(choice, axis=0) > 0.5
    updated = jnp.where(listed[None, :, None], placed, stacked)
    new_east = updated[:level_count]
    new_north = updated[level_count:]

    carried = new_north * cosine[None, :, None]
    v_north, v_south, u_east, u_west = halos(
        carried[:, 0, :], carried[:, -1, :], new_east[:, :, 0], new_east[:, :, -1]
    )
    east_u, west_u = shifted(new_east, u_west[:, :, None], u_east[:, :, None], 2)
    north_v, south_v = shifted(carried, v_south[:, None, :], v_north[:, None, :], 1)
    divergence = (
        lat_factor * (east_u - west_u) * 0.5
        + 0.3 * (north_v - south_v) * 0.5 / cosine[None, :, None]
    )
    new_pressure = pressure - sound_squared[:, None, None] * divergence / column_mass[None]
    return (new_east, new_north, new_pressure)


def solution(mesh):
    in_specs = (
        P(None, "lat", "lon"),
        P(None, "lat", "lon"),
        P(None, "lat", "lon"),
        P(),
        P("lat", "lon"),
        P(),
        P(),
    )
    out_specs = (P(None, "lat", "lon"), P(None, "lat", "lon"), P(None, "lat", "lon"))
    return jax.shard_map(
        on_device, mesh=mesh, in_specs=in_specs, out_specs=out_specs, check_vma=False
    )
```

```python
import jax
import jax.numpy as jnp
from jax import lax
from jax.sharding import PartitionSpec as P

PRECISE = lax.Precision.HIGHEST
SPECTRAL = lax.Precision.HIGH


def shift_pairs(peers, step, wrap):
    pairs = []
    for i in range(peers):
        j = i + step
        if wrap:
            pairs.append((i, j % peers))
        elif 0 <= j < peers:
            pairs.append((i, j))
    return pairs


def halos(lat_first, lat_last, lon_first, lon_last):
    bands = lax.axis_size("lat")
    segs = lax.axis_size("lon")
    north = lax.ppermute(lat_first, "lat", shift_pairs(bands, -1, False))
    south = lax.ppermute(lat_last, "lat", shift_pairs(bands, 1, False))
    east = lax.ppermute(lon_first, "lon", shift_pairs(segs, -1, True))
    west = lax.ppermute(lon_last, "lon", shift_pairs(segs, 1, True))
    return north, south, east, west


def latitude_terms(global_rows, total_rows):
    latitude = (-0.5 + (global_rows.astype(jnp.float32) + 0.5) / total_rows) * jnp.pi
    cosine = jnp.cos(latitude)
    courant = 0.3 * jnp.minimum(1.0 / cosine, 2.0)
    return (cosine, courant)


def slot_table(polar_rows, cutoffs, band_number, row_count, slot_count):
    lower = band_number * row_count
    opening = jnp.sum((polar_rows < lower).astype(jnp.int32))
    spare = jnp.full((slot_count,), -1, jnp.int32)
    entries = lax.dynamic_slice(jnp.concatenate([polar_rows, spare]), (opening,), (slot_count,))
    limits = lax.dynamic_slice(jnp.concatenate([cutoffs, spare]), (opening,), (slot_count,))
    local_rows = entries - lower
    present = (local_rows >= 0) & (local_rows < row_count)
    rows = jnp.arange(row_count, dtype=jnp.int32)
    choice = (local_rows[:, None] == rows[None, :]).astype(jnp.float32)
    return (present, choice, limits, local_rows)


def dft_filter(pieces, limits):
    piece_count, row_total, width = pieces.shape
    length = piece_count * width
    inner = 128
    split = width // inner
    outer = length // inner
    outer_ids = jnp.arange(outer, dtype=jnp.int32)
    inner_ids = jnp.arange(inner, dtype=jnp.int32)
    angle_one = (
        2.0 * jnp.pi * (outer_ids[:, None] * outer_ids[None, :] % outer).astype(jnp.float32) / outer
    )
    angle_two = (
        2.0 * jnp.pi * (inner_ids[:, None] * inner_ids[None, :] % inner).astype(jnp.float32) / inner
    )
    angle_twist = (
        2.0
        * jnp.pi
        * (outer_ids[:, None] * inner_ids[None, :] % length).astype(jnp.float32)
        / length
    )
    cos_one, sin_one = (jnp.cos(angle_one), jnp.sin(angle_one))
    cos_two, sin_two = (jnp.cos(angle_two), jnp.sin(angle_two))
    cos_twist = jnp.cos(angle_twist)[:, None, :]
    sin_twist = jnp.sin(angle_twist)[:, None, :]
    first = jnp.concatenate([cos_one, -sin_one], axis=1)
    forward = jnp.concatenate(
        [jnp.concatenate([cos_two, -sin_two], axis=1), jnp.concatenate([sin_two, cos_two], axis=1)],
        axis=0,
    )
    backward = jnp.concatenate(
        [jnp.concatenate([cos_two, sin_two], axis=1), jnp.concatenate([-sin_two, cos_two], axis=1)],
        axis=0,
    )
    last = jnp.concatenate([cos_one, -sin_one], axis=0)
    spectrum = 0.0
    for part in range(split):
        block = pieces[:, :, part * inner:(part + 1) * inner]
        spectrum = spectrum + jnp.einsum(
            "sqb,sk->kqb", block, first[part::split], precision=SPECTRAL
        )
    real_a = spectrum[:outer]
    imag_a = spectrum[outer:]
    real_b = real_a * cos_twist + imag_a * sin_twist
    imag_b = imag_a * cos_twist - real_a * sin_twist
    mixed = jnp.einsum(
        "kqb,bj->kqj", jnp.concatenate([real_b, imag_b], axis=2), forward, precision=SPECTRAL
    )
    wave_ids = outer_ids[:, None] + outer * inner_ids[None, :]
    wave_ids = jnp.minimum(wave_ids, length - wave_ids)
    keeping = (wave_ids[:, None, :] <= limits[None, :, None]).astype(jnp.float32)
    mixed = mixed * jnp.concatenate([keeping, keeping], axis=2)
    back = jnp.einsum("kqj,jb->kqb", mixed, backward, precision=SPECTRAL)
    real_d = back[:, :, :inner]
    imag_d = back[:, :, inner:]
    real_e = real_d * cos_twist - imag_d * sin_twist
    imag_e = imag_d * cos_twist + real_d * sin_twist
    stacked = jnp.concatenate([real_e, imag_e], axis=0)
    parts = []
    for part in range(split):
        parts.append(
            jnp.einsum("kqb,ks->sqb", stacked, last[:, part::split], precision=SPECTRAL)
        )
    return jnp.concatenate(parts, axis=2) / length


def filter_round(slots, slot_limits):
    field_count, slot_total, seg_width = slots.shape
    peers = lax.axis_size("lon")
    items = slots.reshape(peers, field_count * slot_total // peers, seg_width)
    pieces = lax.all_to_all(items, "lon", split_axis=0, concat_axis=0, tiled=True)
    share = pieces.shape[1]
    item_ids = lax.axis_index("lon") * share + jnp.arange(share, dtype=jnp.int32)
    item_limits = jnp.take(slot_limits, item_ids % slot_total)
    filtered = dft_filter(pieces, item_limits)
    returned = lax.all_to_all(filtered, "lon", split_axis=0, concat_axis=0, tiled=True)
    return returned.reshape(field_count, slot_total, seg_width)


def shifted(block, before, after, axis):
    length = block.shape[axis]
    plus = jnp.concatenate([lax.slice_in_dim(block, 1, length, axis=axis), after], axis=axis)
    minus = jnp.concatenate([before, lax.slice_in_dim(block, 0, length - 1, axis=axis)], axis=axis)
    return plus, minus


def on_device(east_wind, north_wind, pressure, sound_squared, column_mass, polar_rows, cutoffs):
    level_count, row_count, seg_width = pressure.shape
    band_count = lax.axis_size("lat")
    band_number = lax.axis_index("lat")
    total_rows = row_count * band_count
    global_rows = band_number * row_count + jnp.arange(row_count, dtype=jnp.int32)
    cosine, courant = latitude_terms(global_rows, total_rows)
    lat_factor = courant[None, :, None]

    p_north, p_south, p_east, p_west = halos(
        pressure[:, 0, :], pressure[:, -1, :], pressure[:, :, 0], pressure[:, :, -1]
    )
    east, west = shifted(pressure, p_west[:, :, None], p_east[:, :, None], 2)
    north, south = shifted(pressure, p_south[:, None, :], p_north[:, None, :], 1)
    east_step = east_wind - lat_factor * (east - west) * 0.5
    north_step = north_wind - 0.3 * (north - south) * 0.5

    slot_count = row_count // 2
    present, choice, limits, local_rows = slot_table(
        polar_rows, cutoffs, band_number, row_count, slot_count
    )
    rows = jnp.arange(row_count, dtype=jnp.int32)
    above = (local_rows[:, None] + 1 == rows[None, :]).astype(jnp.float32)
    below = (local_rows[:, None] - 1 == rows[None, :]).astype(jnp.float32)
    top = (local_rows == row_count - 1)[None, :, None]
    bottom = (local_rows == 0)[None, :, None]

    def gather(weights, block):
        return jnp.einsum("sr,lrc->lsc", weights, block, precision=PRECISE)

    p_rows = gather(choice, pressure)
    pe_rows = jnp.einsum("sr,lr->ls", choice, p_east, precision=PRECISE)
    pw_rows = jnp.einsum("sr,lr->ls", choice, p_west, precision=PRECISE)
    cour_rows = jnp.einsum("sr,r->s", choice, courant, precision=PRECISE)
    pn_rows = gather(above, pressure) + jnp.where(top, p_north[:, None, :], 0.0)
    ps_rows = gather(below, pressure) + jnp.where(bottom, p_south[:, None, :], 0.0)
    east_r, west_r = shifted(p_rows, pw_rows[:, :, None], pe_rows[:, :, None], 2)
    east_rows = gather(choice, east_wind) - cour_rows[None, :, None] * (east_r - west_r) * 0.5
    north_rows = gather(choice, north_wind) - 0.3 * (pn_rows - ps_rows) * 0.5
    picked = jnp.concatenate([east_rows, north_rows], axis=0)
    stacked = jnp.concatenate([east_step, north_step], axis=0)
    whole_limit = seg_width * lax.axis_size("lon") // 2
    smoothed = filter_round(picked, jnp.where(present, limits, whole_limit))
    fanned = jnp.broadcast_to(choice[None], (2 * level_count,) + choice.shape)
    placed = jnp.einsum("fsr,fsc->frc", fanned, smoothed, precision=PRECISE)
    listed = jnp.sum(choice, axis=0) > 0.5
    updated = jnp.where(listed[None, :, None], placed, stacked)
    new_east = updated[:level_count]
    new_north = updated[level_count:]

    carried = new_north * cosine[None, :, None]
    v_north, v_south, u_east, u_west = halos(
        carried[:, 0, :], carried[:, -1, :], new_east[:, :, 0], new_east[:, :, -1]
    )
    east_u, west_u = shifted(new_east, u_west[:, :, None], u_east[:, :, None], 2)
    north_v, south_v = shifted(carried, v_south[:, None, :], v_north[:, None, :], 1)
    divergence = (
        lat_factor * (east_u - west_u) * 0.5
        + 0.3 * (north_v - south_v) * 0.5 / cosine[None, :, None]
    )
    new_pressure = pressure - sound_squared[:, None, None] * divergence / column_mass[None]
    return (new_east, new_north, new_pressure)


def solution(mesh):
    in_specs = (
        P(None, "lat", "lon"),
        P(None, "lat", "lon"),
        P(None, "lat", "lon"),
        P(),
        P("lat", "lon"),
        P(),
        P(),
    )
    out_specs = (P(None, "lat", "lon"), P(None, "lat", "lon"), P(None, "lat", "lon"))
    return jax.shard_map(
        on_device, mesh=mesh, in_specs=in_specs, out_specs=out_specs, check_vma=False
    )
```

```python
import jax
import jax.numpy as jnp
from jax import lax
from jax.sharding import PartitionSpec as P

PRECISE = lax.Precision.HIGH
SPECTRAL = lax.Precision.HIGH


def shift_pairs(peers, step, wrap):
    pairs = []
    for i in range(peers):
        j = i + step
        if wrap:
            pairs.append((i, j % peers))
        elif 0 <= j < peers:
            pairs.append((i, j))
    return pairs


def halos(lat_first, lat_last, lon_first, lon_last):
    bands = lax.axis_size("lat")
    segs = lax.axis_size("lon")
    north = lax.ppermute(lat_first, "lat", shift_pairs(bands, -1, False))
    south = lax.ppermute(lat_last, "lat", shift_pairs(bands, 1, False))
    east = lax.ppermute(lon_first, "lon", shift_pairs(segs, -1, True))
    west = lax.ppermute(lon_last, "lon", shift_pairs(segs, 1, True))
    return north, south, east, west


def latitude_terms(global_rows, total_rows):
    latitude = (-0.5 + (global_rows.astype(jnp.float32) + 0.5) / total_rows) * jnp.pi
    cosine = jnp.cos(latitude)
    courant = 0.3 * jnp.minimum(1.0 / cosine, 2.0)
    return (cosine, courant)


def slot_table(polar_rows, cutoffs, band_number, row_count, slot_count):
    lower = band_number * row_count
    opening = jnp.sum((polar_rows < lower).astype(jnp.int32))
    spare = jnp.full((slot_count,), -1, jnp.int32)
    entries = lax.dynamic_slice(jnp.concatenate([polar_rows, spare]), (opening,), (slot_count,))
    limits = lax.dynamic_slice(jnp.concatenate([cutoffs, spare]), (opening,), (slot_count,))
    local_rows = entries - lower
    present = (local_rows >= 0) & (local_rows < row_count)
    rows = jnp.arange(row_count, dtype=jnp.int32)
    choice = (local_rows[:, None] == rows[None, :]).astype(jnp.float32)
    return (present, choice, limits, local_rows)


def dft_filter(pieces, limits):
    piece_count, row_total, width = pieces.shape
    length = piece_count * width
    inner = 128
    split = width // inner
    outer = length // inner
    outer_ids = jnp.arange(outer, dtype=jnp.int32)
    inner_ids = jnp.arange(inner, dtype=jnp.int32)
    angle_one = (
        2.0 * jnp.pi * (outer_ids[:, None] * outer_ids[None, :] % outer).astype(jnp.float32) / outer
    )
    angle_two = (
        2.0 * jnp.pi * (inner_ids[:, None] * inner_ids[None, :] % inner).astype(jnp.float32) / inner
    )
    angle_twist = (
        2.0
        * jnp.pi
        * (outer_ids[:, None] * inner_ids[None, :] % length).astype(jnp.float32)
        / length
    )
    cos_one, sin_one = (jnp.cos(angle_one), jnp.sin(angle_one))
    cos_two, sin_two = (jnp.cos(angle_two), jnp.sin(angle_two))
    cos_twist = jnp.cos(angle_twist)[:, None, :]
    sin_twist = jnp.sin(angle_twist)[:, None, :]
    first = jnp.concatenate([cos_one, -sin_one], axis=1)
    forward = jnp.concatenate(
        [jnp.concatenate([cos_two, -sin_two], axis=1), jnp.concatenate([sin_two, cos_two], axis=1)],
        axis=0,
    )
    backward = jnp.concatenate(
        [jnp.concatenate([cos_two, sin_two], axis=1), jnp.concatenate([-sin_two, cos_two], axis=1)],
        axis=0,
    )
    last = jnp.concatenate([cos_one, -sin_one], axis=0)
    spectrum = 0.0
    for part in range(split):
        block = pieces[:, :, part * inner:(part + 1) * inner]
        spectrum = spectrum + jnp.einsum(
            "sqb,sk->kqb", block, first[part::split], precision=SPECTRAL
        )
    real_a = spectrum[:outer]
    imag_a = spectrum[outer:]
    real_b = real_a * cos_twist + imag_a * sin_twist
    imag_b = imag_a * cos_twist - real_a * sin_twist
    mixed = jnp.einsum(
        "kqb,bj->kqj", jnp.concatenate([real_b, imag_b], axis=2), forward, precision=SPECTRAL
    )
    wave_ids = outer_ids[:, None] + outer * inner_ids[None, :]
    wave_ids = jnp.minimum(wave_ids, length - wave_ids)
    keeping = (wave_ids[:, None, :] <= limits[None, :, None]).astype(jnp.float32)
    mixed = mixed * jnp.concatenate([keeping, keeping], axis=2)
    back = jnp.einsum("kqj,jb->kqb", mixed, backward, precision=SPECTRAL)
    real_d = back[:, :, :inner]
    imag_d = back[:, :, inner:]
    real_e = real_d * cos_twist - imag_d * sin_twist
    imag_e = imag_d * cos_twist + real_d * sin_twist
    stacked = jnp.concatenate([real_e, imag_e], axis=0)
    parts = []
    for part in range(split):
        parts.append(
            jnp.einsum("kqb,ks->sqb", stacked, last[:, part::split], precision=SPECTRAL)
        )
    return jnp.concatenate(parts, axis=2) / length


def filter_round(slots, slot_limits):
    field_count, slot_total, seg_width = slots.shape
    peers = lax.axis_size("lon")
    items = slots.reshape(peers, field_count * slot_total // peers, seg_width)
    pieces = lax.all_to_all(items, "lon", split_axis=0, concat_axis=0, tiled=True)
    share = pieces.shape[1]
    item_ids = lax.axis_index("lon") * share + jnp.arange(share, dtype=jnp.int32)
    item_limits = jnp.take(slot_limits, item_ids % slot_total)
    filtered = dft_filter(pieces, item_limits)
    returned = lax.all_to_all(filtered, "lon", split_axis=0, concat_axis=0, tiled=True)
    return returned.reshape(field_count, slot_total, seg_width)


def shifted(block, before, after, axis):
    length = block.shape[axis]
    plus = jnp.concatenate([lax.slice_in_dim(block, 1, length, axis=axis), after], axis=axis)
    minus = jnp.concatenate([before, lax.slice_in_dim(block, 0, length - 1, axis=axis)], axis=axis)
    return plus, minus


def on_device(east_wind, north_wind, pressure, sound_squared, column_mass, polar_rows, cutoffs):
    level_count, row_count, seg_width = pressure.shape
    band_count = lax.axis_size("lat")
    band_number = lax.axis_index("lat")
    total_rows = row_count * band_count
    global_rows = band_number * row_count + jnp.arange(row_count, dtype=jnp.int32)
    cosine, courant = latitude_terms(global_rows, total_rows)
    lat_factor = courant[None, :, None]

    p_north, p_south, p_east, p_west = halos(
        pressure[:, 0, :], pressure[:, -1, :], pressure[:, :, 0], pressure[:, :, -1]
    )
    east, west = shifted(pressure, p_west[:, :, None], p_east[:, :, None], 2)
    north, south = shifted(pressure, p_south[:, None, :], p_north[:, None, :], 1)
    east_step = east_wind - lat_factor * (east - west) * 0.5
    north_step = north_wind - 0.3 * (north - south) * 0.5

    slot_count = row_count // 2
    present, choice, limits, local_rows = slot_table(
        polar_rows, cutoffs, band_number, row_count, slot_count
    )
    rows = jnp.arange(row_count, dtype=jnp.int32)
    above = (local_rows[:, None] + 1 == rows[None, :]).astype(jnp.float32)
    below = (local_rows[:, None] - 1 == rows[None, :]).astype(jnp.float32)
    top = (local_rows == row_count - 1)[None, :, None]
    bottom = (local_rows == 0)[None, :, None]

    def gather(weights, block):
        return jnp.einsum("sr,lrc->lsc", weights, block, precision=PRECISE)

    p_rows = gather(choice, pressure)
    pe_rows = jnp.einsum("sr,lr->ls", choice, p_east, precision=PRECISE)
    pw_rows = jnp.einsum("sr,lr->ls", choice, p_west, precision=PRECISE)
    cour_rows = jnp.einsum("sr,r->s", choice, courant, precision=PRECISE)
    pn_rows = gather(above, pressure) + jnp.where(top, p_north[:, None, :], 0.0)
    ps_rows = gather(below, pressure) + jnp.where(bottom, p_south[:, None, :], 0.0)
    east_r, west_r = shifted(p_rows, pw_rows[:, :, None], pe_rows[:, :, None], 2)
    east_rows = gather(choice, east_wind) - cour_rows[None, :, None] * (east_r - west_r) * 0.5
    north_rows = gather(choice, north_wind) - 0.3 * (pn_rows - ps_rows) * 0.5
    picked = jnp.concatenate([east_rows, north_rows], axis=0)
    stacked = jnp.concatenate([east_step, north_step], axis=0)
    whole_limit = seg_width * lax.axis_size("lon") // 2
    smoothed = filter_round(picked, jnp.where(present, limits, whole_limit))
    fanned = jnp.broadcast_to(choice[None], (2 * level_count,) + choice.shape)
    placed = jnp.einsum("fsr,fsc->frc", fanned, smoothed, precision=PRECISE)
    listed = jnp.sum(choice, axis=0) > 0.5
    updated = jnp.where(listed[None, :, None], placed, stacked)
    new_east = updated[:level_count]
    new_north = updated[level_count:]

    carried = new_north * cosine[None, :, None]
    v_north, v_south, u_east, u_west = halos(
        carried[:, 0, :], carried[:, -1, :], new_east[:, :, 0], new_east[:, :, -1]
    )
    east_u, west_u = shifted(new_east, u_west[:, :, None], u_east[:, :, None], 2)
    north_v, south_v = shifted(carried, v_south[:, None, :], v_north[:, None, :], 1)
    divergence = (
        lat_factor * (east_u - west_u) * 0.5
        + 0.3 * (north_v - south_v) * 0.5 / cosine[None, :, None]
    )
    new_pressure = pressure - sound_squared[:, None, None] * divergence / column_mass[None]
    return (new_east, new_north, new_pressure)


def solution(mesh):
    in_specs = (
        P(None, "lat", "lon"),
        P(None, "lat", "lon"),
        P(None, "lat", "lon"),
        P(),
        P("lat", "lon"),
        P(),
        P(),
    )
    out_specs = (P(None, "lat", "lon"), P(None, "lat", "lon"), P(None, "lat", "lon"))
    return jax.shard_map(
        on_device, mesh=mesh, in_specs=in_specs, out_specs=out_specs, check_vma=False
    )
```

```python
import jax
import jax.numpy as jnp
from jax import lax
from jax.sharding import PartitionSpec as P

PRECISE = lax.Precision.HIGH
SPECTRAL = lax.Precision.HIGH


def shift_pairs(peers, step, wrap):
    pairs = []
    for i in range(peers):
        j = i + step
        if wrap:
            pairs.append((i, j % peers))
        elif 0 <= j < peers:
            pairs.append((i, j))
    return pairs


def halos(lat_first, lat_last, lon_first, lon_last):
    bands = lax.axis_size("lat")
    segs = lax.axis_size("lon")
    north = lax.ppermute(lat_first, "lat", shift_pairs(bands, -1, False))
    south = lax.ppermute(lat_last, "lat", shift_pairs(bands, 1, False))
    east = lax.ppermute(lon_first, "lon", shift_pairs(segs, -1, True))
    west = lax.ppermute(lon_last, "lon", shift_pairs(segs, 1, True))
    return north, south, east, west


def latitude_terms(global_rows, total_rows):
    latitude = (-0.5 + (global_rows.astype(jnp.float32) + 0.5) / total_rows) * jnp.pi
    cosine = jnp.cos(latitude)
    courant = 0.3 * jnp.minimum(1.0 / cosine, 2.0)
    return (cosine, courant)


def slot_table(polar_rows, cutoffs, band_number, row_count, slot_count):
    lower = band_number * row_count
    opening = jnp.sum((polar_rows < lower).astype(jnp.int32))
    spare = jnp.full((slot_count,), -1, jnp.int32)
    entries = lax.dynamic_slice(jnp.concatenate([polar_rows, spare]), (opening,), (slot_count,))
    limits = lax.dynamic_slice(jnp.concatenate([cutoffs, spare]), (opening,), (slot_count,))
    local_rows = entries - lower
    present = (local_rows >= 0) & (local_rows < row_count)
    rows = jnp.arange(row_count, dtype=jnp.int32)
    choice = (local_rows[:, None] == rows[None, :]).astype(jnp.float32)
    return (present, choice, limits, local_rows)


def dft_filter(pieces, limits):
    piece_count, row_total, width = pieces.shape
    length = piece_count * width
    inner = 128
    split = width // inner
    outer = length // inner
    outer_ids = jnp.arange(outer, dtype=jnp.int32)
    inner_ids = jnp.arange(inner, dtype=jnp.int32)
    angle_one = (
        2.0 * jnp.pi * (outer_ids[:, None] * outer_ids[None, :] % outer).astype(jnp.float32) / outer
    )
    angle_two = (
        2.0 * jnp.pi * (inner_ids[:, None] * inner_ids[None, :] % inner).astype(jnp.float32) / inner
    )
    angle_twist = (
        2.0
        * jnp.pi
        * (outer_ids[:, None] * inner_ids[None, :] % length).astype(jnp.float32)
        / length
    )
    cos_one, sin_one = (jnp.cos(angle_one), jnp.sin(angle_one))
    cos_two, sin_two = (jnp.cos(angle_two), jnp.sin(angle_two))
    cos_twist = jnp.cos(angle_twist)[:, None, :]
    sin_twist = jnp.sin(angle_twist)[:, None, :]
    first = jnp.concatenate([cos_one, -sin_one], axis=1)
    forward = jnp.concatenate(
        [jnp.concatenate([cos_two, -sin_two], axis=1), jnp.concatenate([sin_two, cos_two], axis=1)],
        axis=0,
    )
    backward = jnp.concatenate(
        [jnp.concatenate([cos_two, sin_two], axis=1), jnp.concatenate([-sin_two, cos_two], axis=1)],
        axis=0,
    )
    last = jnp.concatenate([cos_one, -sin_one], axis=0)
    spectrum = 0.0
    for part in range(split):
        block = pieces[:, :, part * inner:(part + 1) * inner]
        spectrum = spectrum + jnp.einsum(
            "sqb,sk->kqb", block, first[part::split], precision=SPECTRAL
        )
    real_a = spectrum[:outer]
    imag_a = spectrum[outer:]
    real_b = real_a * cos_twist + imag_a * sin_twist
    imag_b = imag_a * cos_twist - real_a * sin_twist
    mixed = jnp.einsum(
        "kqb,bj->kqj", jnp.concatenate([real_b, imag_b], axis=2), forward, precision=SPECTRAL
    )
    wave_ids = outer_ids[:, None] + outer * inner_ids[None, :]
    wave_ids = jnp.minimum(wave_ids, length - wave_ids)
    keeping = (wave_ids[:, None, :] <= limits[None, :, None]).astype(jnp.float32)
    mixed = mixed * jnp.concatenate([keeping, keeping], axis=2)
    back = jnp.einsum("kqj,jb->kqb", mixed, backward, precision=SPECTRAL)
    real_d = back[:, :, :inner]
    imag_d = back[:, :, inner:]
    real_e = real_d * cos_twist - imag_d * sin_twist
    imag_e = imag_d * cos_twist + real_d * sin_twist
    stacked = jnp.concatenate([real_e, imag_e], axis=0)
    parts = []
    for part in range(split):
        parts.append(
            jnp.einsum("kqb,ks->sqb", stacked, last[:, part::split], precision=SPECTRAL)
        )
    return jnp.concatenate(parts, axis=2) / length


def filter_round(slots, slot_limits):
    field_count, slot_total, seg_width = slots.shape
    peers = lax.axis_size("lon")
    items = slots.reshape(peers, field_count * slot_total // peers, seg_width)
    pieces = lax.all_to_all(items, "lon", split_axis=0, concat_axis=0, tiled=True)
    share = pieces.shape[1]
    start = (lax.axis_index("lon") * share) % slot_total
    item_limits = lax.dynamic_slice(slot_limits, (start,), (share,))
    filtered = dft_filter(pieces, item_limits)
    returned = lax.all_to_all(filtered, "lon", split_axis=0, concat_axis=0, tiled=True)
    return returned.reshape(field_count, slot_total, seg_width)


def shifted(block, before, after, axis):
    length = block.shape[axis]
    plus = jnp.concatenate([lax.slice_in_dim(block, 1, length, axis=axis), after], axis=axis)
    minus = jnp.concatenate([before, lax.slice_in_dim(block, 0, length - 1, axis=axis)], axis=axis)
    return plus, minus


def on_device(east_wind, north_wind, pressure, sound_squared, column_mass, polar_rows, cutoffs):
    level_count, row_count, seg_width = pressure.shape
    band_count = lax.axis_size("lat")
    band_number = lax.axis_index("lat")
    total_rows = row_count * band_count
    global_rows = band_number * row_count + jnp.arange(row_count, dtype=jnp.int32)
    cosine, courant = latitude_terms(global_rows, total_rows)
    lat_factor = courant[None, :, None]

    p_north, p_south, p_east, p_west = halos(
        pressure[:, 0, :], pressure[:, -1, :], pressure[:, :, 0], pressure[:, :, -1]
    )
    east, west = shifted(pressure, p_west[:, :, None], p_east[:, :, None], 2)
    north, south = shifted(pressure, p_south[:, None, :], p_north[:, None, :], 1)
    east_step = east_wind - lat_factor * (east - west) * 0.5
    north_step = north_wind - 0.3 * (north - south) * 0.5

    slot_count = row_count // 2
    present, choice, limits, local_rows = slot_table(
        polar_rows, cutoffs, band_number, row_count, slot_count
    )
    rows = jnp.arange(row_count, dtype=jnp.int32)
    above = (local_rows[:, None] + 1 == rows[None, :]).astype(jnp.float32)
    below = (local_rows[:, None] - 1 == rows[None, :]).astype(jnp.float32)
    top = (local_rows == row_count - 1)[None, :, None]
    bottom = (local_rows == 0)[None, :, None]

    def gather(weights, block):
        return jnp.einsum("sr,lrc->lsc", weights, block, precision=PRECISE)

    p_rows = gather(choice, pressure)
    pe_rows = jnp.einsum("sr,lr->ls", choice, p_east, precision=PRECISE)
    pw_rows = jnp.einsum("sr,lr->ls", choice, p_west, precision=PRECISE)
    cour_rows = jnp.einsum("sr,r->s", choice, courant, precision=PRECISE)
    pn_rows = gather(above, pressure) + jnp.where(top, p_north[:, None, :], 0.0)
    ps_rows = gather(below, pressure) + jnp.where(bottom, p_south[:, None, :], 0.0)
    east_r, west_r = shifted(p_rows, pw_rows[:, :, None], pe_rows[:, :, None], 2)
    east_rows = gather(choice, east_wind) - cour_rows[None, :, None] * (east_r - west_r) * 0.5
    north_rows = gather(choice, north_wind) - 0.3 * (pn_rows - ps_rows) * 0.5
    picked = jnp.concatenate([east_rows, north_rows], axis=0)
    stacked = jnp.concatenate([east_step, north_step], axis=0)
    whole_limit = seg_width * lax.axis_size("lon") // 2
    smoothed = filter_round(picked, jnp.where(present, limits, whole_limit))
    fanned = jnp.broadcast_to(choice[None], (2 * level_count,) + choice.shape)
    placed = jnp.einsum("fsr,fsc->frc", fanned, smoothed, precision=PRECISE)
    listed = jnp.sum(choice, axis=0) > 0.5
    updated = jnp.where(listed[None, :, None], placed, stacked)
    new_east = updated[:level_count]
    new_north = updated[level_count:]

    carried = new_north * cosine[None, :, None]
    v_north, v_south, u_east, u_west = halos(
        carried[:, 0, :], carried[:, -1, :], new_east[:, :, 0], new_east[:, :, -1]
    )
    east_u, west_u = shifted(new_east, u_west[:, :, None], u_east[:, :, None], 2)
    north_v, south_v = shifted(carried, v_south[:, None, :], v_north[:, None, :], 1)
    divergence = (
        lat_factor * (east_u - west_u) * 0.5
        + 0.3 * (north_v - south_v) * 0.5 / cosine[None, :, None]
    )
    new_pressure = pressure - sound_squared[:, None, None] * divergence / column_mass[None]
    return (new_east, new_north, new_pressure)


def solution(mesh):
    in_specs = (
        P(None, "lat", "lon"),
        P(None, "lat", "lon"),
        P(None, "lat", "lon"),
        P(),
        P("lat", "lon"),
        P(),
        P(),
    )
    out_specs = (P(None, "lat", "lon"), P(None, "lat", "lon"), P(None, "lat", "lon"))
    return jax.shard_map(
        on_device, mesh=mesh, in_specs=in_specs, out_specs=out_specs, check_vma=False
    )
```

```python
import jax
import jax.numpy as jnp
from jax import lax
from jax.sharding import PartitionSpec as P

PRECISE = lax.Precision.HIGH
SPECTRAL = lax.Precision.HIGH


def shift_pairs(peers, step, wrap):
    pairs = []
    for i in range(peers):
        j = i + step
        if wrap:
            pairs.append((i, j % peers))
        elif 0 <= j < peers:
            pairs.append((i, j))
    return pairs


def halos(lat_first, lat_last, lon_first, lon_last):
    bands = lax.axis_size("lat")
    segs = lax.axis_size("lon")
    north = lax.ppermute(lat_first, "lat", shift_pairs(bands, -1, False))
    south = lax.ppermute(lat_last, "lat", shift_pairs(bands, 1, False))
    east = lax.ppermute(lon_first, "lon", shift_pairs(segs, -1, True))
    west = lax.ppermute(lon_last, "lon", shift_pairs(segs, 1, True))
    return north, south, east, west


def latitude_terms(global_rows, total_rows):
    latitude = (-0.5 + (global_rows.astype(jnp.float32) + 0.5) / total_rows) * jnp.pi
    cosine = jnp.cos(latitude)
    courant = 0.3 * jnp.minimum(1.0 / cosine, 2.0)
    return (cosine, courant)


def slot_table(polar_rows, cutoffs, band_number, row_count, slot_count):
    lower = band_number * row_count
    opening = jnp.sum((polar_rows < lower).astype(jnp.int32))
    spare = jnp.full((slot_count,), -1, jnp.int32)
    entries = lax.dynamic_slice(jnp.concatenate([polar_rows, spare]), (opening,), (slot_count,))
    limits = lax.dynamic_slice(jnp.concatenate([cutoffs, spare]), (opening,), (slot_count,))
    local_rows = entries - lower
    present = (local_rows >= 0) & (local_rows < row_count)
    rows = jnp.arange(row_count, dtype=jnp.int32)
    choice = (local_rows[:, None] == rows[None, :]).astype(jnp.float32)
    return (present, choice, limits, local_rows)


def dft_filter(pieces, limits):
    piece_count, row_total, width = pieces.shape
    length = piece_count * width
    inner = 128
    split = width // inner
    outer = length // inner
    outer_ids = jnp.arange(outer, dtype=jnp.int32)
    inner_ids = jnp.arange(inner, dtype=jnp.int32)
    angle_one = (
        2.0 * jnp.pi * (outer_ids[:, None] * outer_ids[None, :] % outer).astype(jnp.float32) / outer
    )
    angle_two = (
        2.0 * jnp.pi * (inner_ids[:, None] * inner_ids[None, :] % inner).astype(jnp.float32) / inner
    )
    angle_twist = (
        2.0
        * jnp.pi
        * (outer_ids[:, None] * inner_ids[None, :] % length).astype(jnp.float32)
        / length
    )
    cos_one, sin_one = (jnp.cos(angle_one), jnp.sin(angle_one))
    cos_two, sin_two = (jnp.cos(angle_two), jnp.sin(angle_two))
    cos_twist = jnp.cos(angle_twist)[:, None, :]
    sin_twist = jnp.sin(angle_twist)[:, None, :]
    first = jnp.concatenate([cos_one, -sin_one], axis=1)
    forward = jnp.concatenate(
        [jnp.concatenate([cos_two, -sin_two], axis=1), jnp.concatenate([sin_two, cos_two], axis=1)],
        axis=0,
    )
    backward = jnp.concatenate(
        [jnp.concatenate([cos_two, sin_two], axis=1), jnp.concatenate([-sin_two, cos_two], axis=1)],
        axis=0,
    )
    last = jnp.concatenate([cos_one, -sin_one], axis=0) / length
    spectrum = 0.0
    for part in range(split):
        block = pieces[:, :, part * inner:(part + 1) * inner]
        spectrum = spectrum + jnp.einsum(
            "sqb,sk->kqb", block, first[part::split], precision=SPECTRAL
        )
    real_a = spectrum[:outer]
    imag_a = spectrum[outer:]
    real_b = real_a * cos_twist + imag_a * sin_twist
    imag_b = imag_a * cos_twist - real_a * sin_twist
    mixed = jnp.einsum(
        "kqb,bj->kqj", jnp.concatenate([real_b, imag_b], axis=2), forward, precision=SPECTRAL
    )
    wave_ids = outer_ids[:, None] + outer * inner_ids[None, :]
    wave_ids = jnp.minimum(wave_ids, length - wave_ids)
    keeping = (wave_ids[:, None, :] <= limits[None, :, None]).astype(jnp.float32)
    mixed = mixed * jnp.concatenate([keeping, keeping], axis=2)
    back = jnp.einsum("kqj,jb->kqb", mixed, backward, precision=SPECTRAL)
    real_d = back[:, :, :inner]
    imag_d = back[:, :, inner:]
    real_e = real_d * cos_twist - imag_d * sin_twist
    imag_e = imag_d * cos_twist + real_d * sin_twist
    stacked = jnp.concatenate([real_e, imag_e], axis=0)
    parts = []
    for part in range(split):
        parts.append(
            jnp.einsum("kqb,ks->sqb", stacked, last[:, part::split], precision=SPECTRAL)
        )
    return jnp.concatenate(parts, axis=2)


def filter_round(slots, slot_limits):
    field_count, slot_total, seg_width = slots.shape
    peers = lax.axis_size("lon")
    items = slots.reshape(peers, field_count * slot_total // peers, seg_width)
    pieces = lax.all_to_all(items, "lon", split_axis=0, concat_axis=0, tiled=True)
    share = pieces.shape[1]
    start = (lax.axis_index("lon") * share) % slot_total
    item_limits = lax.dynamic_slice(slot_limits, (start,), (share,))
    filtered = dft_filter(pieces, item_limits)
    returned = lax.all_to_all(filtered, "lon", split_axis=0, concat_axis=0, tiled=True)
    return returned.reshape(field_count, slot_total, seg_width)


def shifted(block, before, after, axis):
    length = block.shape[axis]
    plus = jnp.concatenate([lax.slice_in_dim(block, 1, length, axis=axis), after], axis=axis)
    minus = jnp.concatenate([before, lax.slice_in_dim(block, 0, length - 1, axis=axis)], axis=axis)
    return plus, minus


def on_device(east_wind, north_wind, pressure, sound_squared, column_mass, polar_rows, cutoffs):
    level_count, row_count, seg_width = pressure.shape
    band_count = lax.axis_size("lat")
    band_number = lax.axis_index("lat")
    total_rows = row_count * band_count
    global_rows = band_number * row_count + jnp.arange(row_count, dtype=jnp.int32)
    cosine, courant = latitude_terms(global_rows, total_rows)
    lat_factor = courant[None, :, None]

    p_north, p_south, p_east, p_west = halos(
        pressure[:, 0, :], pressure[:, -1, :], pressure[:, :, 0], pressure[:, :, -1]
    )
    east, west = shifted(pressure, p_west[:, :, None], p_east[:, :, None], 2)
    north, south = shifted(pressure, p_south[:, None, :], p_north[:, None, :], 1)
    east_step = east_wind - lat_factor * (east - west) * 0.5
    north_step = north_wind - 0.3 * (north - south) * 0.5

    slot_count = row_count // 2
    present, choice, limits, local_rows = slot_table(
        polar_rows, cutoffs, band_number, row_count, slot_count
    )
    rows = jnp.arange(row_count, dtype=jnp.int32)
    above = (local_rows[:, None] + 1 == rows[None, :]).astype(jnp.float32)
    below = (local_rows[:, None] - 1 == rows[None, :]).astype(jnp.float32)
    top = (local_rows == row_count - 1)[None, :, None]
    bottom = (local_rows == 0)[None, :, None]

    def gather(weights, block):
        return jnp.einsum("sr,lrc->lsc", weights, block, precision=PRECISE)

    p_rows = gather(choice, pressure)
    pe_rows = jnp.einsum("sr,lr->ls", choice, p_east, precision=PRECISE)
    pw_rows = jnp.einsum("sr,lr->ls", choice, p_west, precision=PRECISE)
    cour_rows = jnp.einsum("sr,r->s", choice, courant, precision=PRECISE)
    pn_rows = gather(above, pressure) + jnp.where(top, p_north[:, None, :], 0.0)
    ps_rows = gather(below, pressure) + jnp.where(bottom, p_south[:, None, :], 0.0)
    east_r, west_r = shifted(p_rows, pw_rows[:, :, None], pe_rows[:, :, None], 2)
    east_rows = gather(choice, east_wind) - cour_rows[None, :, None] * (east_r - west_r) * 0.5
    north_rows = gather(choice, north_wind) - 0.3 * (pn_rows - ps_rows) * 0.5
    picked = jnp.concatenate([east_rows, north_rows], axis=0)
    stacked = jnp.concatenate([east_step, north_step], axis=0)
    whole_limit = seg_width * lax.axis_size("lon") // 2
    smoothed = filter_round(picked, jnp.where(present, limits, whole_limit))
    fanned = jnp.broadcast_to(choice[None], (2 * level_count,) + choice.shape)
    placed = jnp.einsum("fsr,fsc->frc", fanned, smoothed, precision=PRECISE)
    listed = jnp.sum(choice, axis=0) > 0.5
    updated = jnp.where(listed[None, :, None], placed, stacked)
    new_east = updated[:level_count]
    new_north = updated[level_count:]

    carried = new_north * cosine[None, :, None]
    v_north, v_south, u_east, u_west = halos(
        carried[:, 0, :], carried[:, -1, :], new_east[:, :, 0], new_east[:, :, -1]
    )
    east_u, west_u = shifted(new_east, u_west[:, :, None], u_east[:, :, None], 2)
    north_v, south_v = shifted(carried, v_south[:, None, :], v_north[:, None, :], 1)
    divergence = (
        lat_factor * (east_u - west_u) * 0.5
        + 0.3 * (north_v - south_v) * 0.5 / cosine[None, :, None]
    )
    new_pressure = pressure - sound_squared[:, None, None] * divergence / column_mass[None]
    return (new_east, new_north, new_pressure)


def solution(mesh):
    in_specs = (
        P(None, "lat", "lon"),
        P(None, "lat", "lon"),
        P(None, "lat", "lon"),
        P(),
        P("lat", "lon"),
        P(),
        P(),
    )
    out_specs = (P(None, "lat", "lon"), P(None, "lat", "lon"), P(None, "lat", "lon"))
    return jax.shard_map(
        on_device, mesh=mesh, in_specs=in_specs, out_specs=out_specs, check_vma=False
    )
```
